256 devices in a mesh: blk: 64 (over y, z, core), lev: 4 (over x).
Axes of the slice: x: 4, y: 4, z: 8, core: 2. Of those that a mesh axis runs over, the one named last changes fastest.
Arguments:
- adjoint_in: float32 [4096, 12, 1024], P('blk', 'lev'), may hold values from -6 to 6
- courant: float32 [2, 4096, 12, 1024], P(None, 'blk', 'lev'), may hold values from 0.05 to 0.45
- mixing: float32 [4096, 12, 1024], P('blk', 'lev'), may hold values from 0.5 to 8
- oh_rate: float32 [4096, 12, 1024], P('blk', 'lev'), may hold values from 0.02 to 0.6
- substeps: int32 [4096], P('blk'), may hold values from 1 to 4
- nest_weight: float32 [4096, 128], P('blk'), may hold values from 0.2 to 0.9
- dest_device: int32 [4096, 1], P('blk'), may hold values from 0 to 63; in each aligned block of 64 rows (0 to 63, 64 to 127, ...) at most 2 rows name the same one
- dest_slot: int32 [4096], P('blk'), may hold values from 0 to 63
- emission_profile: float32 [12], P('lev'), may hold values from 0.05 to 1
- tile_owner: int32 [4096], P('blk'), may hold values from 0 to 1023, as said below
Outputs:
- adjoint_out: float32 [4096, 12, 1024], P('blk', 'lev')
- tile_grad: float32 [1024, 1024], P(('blk', 'lev'))
The draws below stay inside these ranges and needn't reach their ends.
Inputs may be any that keep to these rules, and one draw needn't show every extreme that they name: Of the 64 blocks of one index of blk, at most 2 have the same dest_device. Tiles form 64 groups of 16 consecutive tiles. Of the 64 blocks of one index of blk, at most 2 have tile_owner in the same group, and some group holds exactly 2 of them.
All inputs are finite; a program needn't handle non-finite values.
Results may differ from the reference program's by a relative error of at most 0.0003.
Values sent between devices are 32-bit elements; how exact they have to be, the bound alone decides.
No kernel may reach another device: no remote copies, remote signals or barrier semaphores. Data moves between devices by JAX's collectives and lax.ppermute only.
A program may use at most 128 MiB of HBM per device.

```python
import math
import jax
import jax.numpy as jnp
import numpy as np

NB_DEV = 64
SIDE = 32
RMAX = 4
STEPS = 2
CELLS = 1024
CYCLE = 128
BLOCKS = 4096
LEVELS = 12
CYCLE_PEERS = 64
CAP = 2
TILES = 1024


def owner_rows(sub):
    slot_total = CYCLE_PEERS * CAP
    group_size = NB_DEV // 4
    first, second, third, fourth = jax.random.split(sub, 4)
    scores = jax.random.permutation(first, slot_total).astype(jnp.int32)
    full_group = jax.random.randint(second, (), 0, CYCLE_PEERS).astype(jnp.int32)
    slot_ids = jnp.arange(slot_total, dtype=jnp.int32)
    forced = slot_ids // CAP == full_group
    scores = jnp.where(forced, -1 - slot_ids, scores)
    chosen = jnp.argsort(scores, stable=True)[:NB_DEV].astype(jnp.int32)
    chosen = chosen[jax.random.permutation(fourth, NB_DEV)]
    groups = chosen // CAP
    within = jax.random.randint(third, (NB_DEV,), 0, group_size).astype(jnp.int32)
    return groups * group_size + within


def draw_tile_owner(key, part):
    keys_all = jax.random.split(jax.random.fold_in(key, 71), CYCLE_PEERS)
    return jax.vmap(owner_rows)(keys_all).reshape(BLOCKS).astype(jnp.int32)


def place_ends(values, own_key, least, high):
    dims = values.shape
    place = [jax.random.randint(jax.random.fold_in(own_key, axis), (), 0, dims[axis]) for axis in range(len(dims))]
    values = values.at[tuple(place)].set(least)
    longest = dims.index(max(dims))
    place[longest] = (place[longest] + 1) % dims[longest]
    return values.at[tuple(place)].set(high)


def block_scale(own_key, dims, shards, smallest, largest):
    def one(axis_at, parts):
        draws = jax.random.uniform(jax.random.fold_in(jax.random.fold_in(own_key, 6), axis_at), (parts,), jnp.float32, smallest / len(shards), largest / len(shards))
        return jnp.repeat(jnp.exp(draws), dims[axis_at] // parts).reshape((-1,) + (1,) * (len(dims) - axis_at - 1))

    loudness = one(*shards[0])
    for cut in shards[1:]:
        loudness = loudness * one(*cut)
    return loudness


def deal_out(rng, own, number, rows, count, top, bound, skew):
    ranking = jax.random.permutation(rng, count)
    packed, usual = portions_of(count, rows * top, bound, skew, True), portions_of(count, rows * top, bound, skew, False)
    places = jnp.arange(count)

    def named(lengths, rotation):
        used = int((lengths > 0).sum())
        fixed = max(1, used // 4)
        moved = fixed + (places - fixed + rotation * (used - fixed)) % max(1, count - fixed)
        return jnp.zeros((count,), jnp.int32).at[ranking[jnp.where(places < fixed, places, moved)]].set(jnp.asarray(lengths, jnp.int32))

    lengths = jnp.where(number % 4 == 0, named(packed, number // 4), named(usual, number - number // 4 - 1))
    mixed = jax.random.permutation(jax.random.fold_in(own, 3), count)
    giver, sink = mixed[0:count // 2 * 2:2], mixed[1:count // 2 * 2:2]
    room = jnp.minimum(lengths[giver] - 1, bound - lengths[sink]) // 2
    room = jnp.where((giver == ranking[0]) | (sink == ranking[0]) | (lengths[sink] == 0), 0, jnp.maximum(room, 0))
    moved = jax.random.randint(jax.random.fold_in(own, 4), (count // 2,), 0, 1 << 20) % (room + 1)
    lengths = lengths.at[giver].add(-moved).at[sink].add(moved)
    members = jnp.searchsorted(jnp.cumsum(lengths), jnp.arange(rows * top), side="right").astype(jnp.int32)
    table = members.reshape(top, rows).T
    table = table[jax.random.permutation(jax.random.fold_in(own, 1), rows)]
    rotation = jax.random.randint(jax.random.fold_in(own, 2), (rows, 1), 0, top)
    return jnp.take_along_axis(table, (jnp.arange(top)[None, :] + rotation) % top, axis=1)


def portions_of(amount, total, reach, lean, full):
    portions = [(1 << 20) // math.isqrt(standing ** lean) + 1 for standing in range(1, amount + 1)]
    largest = reach if full else min(reach, max(-(-total // amount), total * portions[0] // sum(portions)))
    least = 1 if total - largest >= amount - 1 else 0
    counts, rest = [largest] + [least] * (amount - 1), total - largest - least * (amount - 1)
    while rest > 0:
        free = [i for i in range(1, amount) if counts[i] < largest] or [i for i in range(1, amount) if counts[i] < reach]
        pool, budget = sum([portions[i] for i in free]), rest
        for i in free:
            extra = min(reach - counts[i], max(1, budget * portions[i] // pool), rest)
            counts[i] = counts[i] + extra
            rest = rest - extra
    return np.array(counts)


def scatter_about(stream_key, dims, spread, most, cuts=(), kind=jnp.bfloat16):
    array = jax.random.normal(stream_key, dims, jnp.float32) * spread
    if len(cuts) > 0:
        array = block_scale(stream_key, dims, cuts, -0.22, 0.18) * array
    return jnp.clip(array, min=-most, max=most).astype(kind)


def setup_inputs(seed: int = 0) -> dict:
    key_list = jax.random.split(jax.random.key(seed), 11)
    adjoint_in = scatter_about(key_list[0], (BLOCKS, LEVELS, CELLS), 1.0, 6.0, ((0, 64), (1, 4)), jnp.float32)
    courant = jnp.clip(0.05 + 0.39999999 * jax.random.uniform(key_list[1], (2, BLOCKS, LEVELS, CELLS), jnp.float32) ** block_scale(key_list[1], (2, BLOCKS, LEVELS, CELLS), ((1, 64), (2, 4)), -0.2, 0.2), 0.05, 0.45)
    mixing = jnp.clip(jnp.exp(math.log(8.0) - 2.7725887 * jax.random.uniform(key_list[2], (BLOCKS, LEVELS, CELLS), jnp.float32) ** block_scale(key_list[2], (BLOCKS, LEVELS, CELLS), ((0, 64), (1, 4)), -0.2, 0.2)), 0.5, 8.0)
    oh_rate = jnp.clip(jnp.exp(math.log(0.6) - 3.4011974 * jax.random.uniform(key_list[3], (BLOCKS, LEVELS, CELLS), jnp.float32) ** block_scale(key_list[3], (BLOCKS, LEVELS, CELLS), ((0, 64), (1, 4)), -0.2, 0.2)), 0.02, 0.6)
    substeps = place_ends(jax.random.randint(key_list[4], (BLOCKS,), 1, RMAX + 1), jax.random.fold_in(key_list[4], 1), 1, RMAX).astype(jnp.int32)
    nest_weight = jnp.clip(0.2 + 0.7 * jax.random.uniform(key_list[5], (BLOCKS, CYCLE), jnp.float32) ** block_scale(key_list[5], (BLOCKS, CYCLE), ((0, 64),), -0.2, 0.2), 0.2, 0.9)
    dest_device_keys = jax.random.split(jax.random.fold_in(key_list[6], 1), BLOCKS // NB_DEV)
    dest_device_turns = jax.random.permutation(jax.random.fold_in(key_list[6], 3), BLOCKS // NB_DEV)
    dest_device = jax.vmap(lambda own, number: deal_out(jax.random.fold_in(key_list[6], 2), own, number, NB_DEV, CYCLE_PEERS, 1, CAP, 2))(dest_device_keys, dest_device_turns).reshape((BLOCKS, 1))
    dest_slot = place_ends(jax.random.randint(key_list[7], (BLOCKS,), 0, NB_DEV), jax.random.fold_in(key_list[7], 1), 0, NB_DEV - 1).astype(jnp.int32)
    emission_profile = jnp.clip(jnp.exp(math.log(1.0) - 2.9957323 * jax.random.uniform(key_list[8], (LEVELS,), jnp.float32) ** block_scale(key_list[8], (LEVELS,), ((0, 4),), -0.2, 0.2)), 0.05, 1.0)
    tile_owner = draw_tile_owner(jax.random.fold_in(key_list[10], 71), 0)
    return {"adjoint_in": adjoint_in, "courant": courant, "mixing": mixing, "oh_rate": oh_rate, "substeps": substeps, "nest_weight": nest_weight, "dest_device": dest_device, "dest_slot": dest_slot, "emission_profile": emission_profile, "tile_owner": tile_owner}


def solve_columns(right_side, coupling):
    level_count = right_side.shape[1]
    ratios = []
    scaled = []
    for level in range(level_count):
        lower_k = coupling[:, level - 1] if level > 0 else 0.0
        upper_k = coupling[:, level] if level < level_count - 1 else 0.0
        diag_term = 1.0 + lower_k + upper_k
        if level == 0:
            pivot_val = diag_term
            scaled.append(right_side[:, 0] / pivot_val)
        else:
            pivot_val = diag_term + lower_k * ratios[level - 1]
            scaled.append((right_side[:, level] + lower_k * scaled[level - 1]) / pivot_val)
        ratios.append(-upper_k / pivot_val)
    solved = [None] * level_count
    solved[level_count - 1] = scaled[level_count - 1]
    for level in range(level_count - 2, -1, -1):
        solved[level] = scaled[level] - ratios[level] * solved[level + 1]
    return jnp.stack(solved, axis=1)


def stencil(adjoint, east_u, north_u, side_len):
    shape_grid = adjoint.shape[:-1] + (side_len, side_len)
    grid_view = adjoint.reshape(shape_grid)
    east_c = east_u.reshape(shape_grid)
    north_c = north_u.reshape(shape_grid)
    zero_col = jnp.zeros(shape_grid[:-1] + (1,), jnp.float32)
    east_adj = jnp.concatenate([grid_view[..., 1:], zero_col], axis=-1)
    zero_row = jnp.zeros(shape_grid[:-2] + (1, side_len), jnp.float32)
    north_adj = jnp.concatenate([grid_view[..., 1:, :], zero_row], axis=-2)
    result = (1.0 - east_c - north_c) * grid_view + east_c * east_adj + north_c * north_adj
    return result.reshape(adjoint.shape)


def faces(adjoint, side_len):
    grid_view = adjoint.reshape(adjoint.shape[:-1] + (side_len, side_len))
    return jnp.concatenate([grid_view[..., 0, :], grid_view[..., side_len - 1, :], grid_view[..., :, 0], grid_view[..., :, side_len - 1]], axis=-1)


def add_faces(adjoint, arrivals, side_len):
    grid_view = adjoint.reshape(adjoint.shape[:-1] + (side_len, side_len))
    grid_view = grid_view.at[..., 0, :].add(arrivals[..., 0:side_len])
    grid_view = grid_view.at[..., side_len - 1, :].add(arrivals[..., side_len:2 * side_len])
    grid_view = grid_view.at[..., :, 0].add(arrivals[..., 2 * side_len:3 * side_len])
    grid_view = grid_view.at[..., :, side_len - 1].add(arrivals[..., 3 * side_len:])
    return grid_view.reshape(adjoint.shape)


def reference(adjoint_in, courant, mixing, oh_rate, substeps, nest_weight, dest_device, dest_slot, emission_profile, tile_owner):
    side_len = SIDE
    survive = jnp.exp(-oh_rate)
    target = (dest_device[:, 0] * NB_DEV + dest_slot).astype(jnp.int32)
    adjoint = adjoint_in
    grad_sum = jnp.zeros((BLOCKS, CELLS), jnp.float32)
    for step_index in range(STEPS):
        grad_sum = grad_sum + jnp.sum(adjoint * emission_profile[None, :, None], axis=1)
        adjoint = solve_columns(adjoint * survive, mixing)
        cycle_out = faces(adjoint, side_len) * nest_weight[:, None, :]
        arrivals = jax.ops.segment_sum(cycle_out, target, num_segments=BLOCKS)
        advected = adjoint
        for substep in range(RMAX):
            active = (substep < substeps)[:, None, None]
            advected = jnp.where(active, stencil(advected, courant[0], courant[1], side_len), advected)
        adjoint = add_faces(advected, arrivals, side_len)
    tile_grad = jax.ops.segment_sum(grad_sum, tile_owner, num_segments=TILES)
    return adjoint, tile_grad
```

```python
import jax
import jax.numpy as jnp
from jax import lax
from jax.sharding import PartitionSpec as P

RMAX = 4
STEPS = 2


def solve_columns(right_side, coupling):
    level_count = right_side.shape[1]
    ratios = []
    scaled = []
    for level in range(level_count):
        lower_k = coupling[:, level - 1] if level > 0 else 0.0
        upper_k = coupling[:, level] if level < level_count - 1 else 0.0
        diag_term = 1.0 + lower_k + upper_k
        if level == 0:
            pivot_val = diag_term
            scaled.append(right_side[:, 0] / pivot_val)
        else:
            pivot_val = diag_term + lower_k * ratios[level - 1]
            scaled.append((right_side[:, level] + lower_k * scaled[level - 1]) / pivot_val)
        ratios.append(-upper_k / pivot_val)
    solved = [None] * level_count
    solved[level_count - 1] = scaled[level_count - 1]
    for level in range(level_count - 2, -1, -1):
        solved[level] = scaled[level] - ratios[level] * solved[level + 1]
    return jnp.stack(solved, axis=1)


def stencil(adjoint, east_u, north_u, side_len):
    shape_grid = adjoint.shape[:-1] + (side_len, side_len)
    grid_view = adjoint.reshape(shape_grid)
    east_c = east_u.reshape(shape_grid)
    north_c = north_u.reshape(shape_grid)
    zero_col = jnp.zeros(shape_grid[:-1] + (1,), jnp.float32)
    east_adj = jnp.concatenate([grid_view[..., 1:], zero_col], axis=-1)
    zero_row = jnp.zeros(shape_grid[:-2] + (1, side_len), jnp.float32)
    north_adj = jnp.concatenate([grid_view[..., 1:, :], zero_row], axis=-2)
    result = (1.0 - east_c - north_c) * grid_view + east_c * east_adj + north_c * north_adj
    return result.reshape(adjoint.shape)


def faces(adjoint, side_len):
    grid_view = adjoint.reshape(adjoint.shape[:-1] + (side_len, side_len))
    return jnp.concatenate(
        [
            grid_view[..., 0, :],
            grid_view[..., side_len - 1, :],
            grid_view[..., :, 0],
            grid_view[..., :, side_len - 1],
        ],
        axis=-1,
    )


def add_faces(adjoint, arrivals, side_len):
    grid_view = adjoint.reshape(adjoint.shape[:-1] + (side_len, side_len))
    grid_view = grid_view.at[..., 0, :].add(arrivals[..., 0:side_len])
    grid_view = grid_view.at[..., side_len - 1, :].add(arrivals[..., side_len : 2 * side_len])
    grid_view = grid_view.at[..., :, 0].add(arrivals[..., 2 * side_len : 3 * side_len])
    grid_view = grid_view.at[..., :, side_len - 1].add(arrivals[..., 3 * side_len :])
    return grid_view.reshape(adjoint.shape)


def pack_plan(keys, dest_count, cap):
    count = keys.shape[0]
    order = jnp.arange(count, dtype=jnp.int32)
    earlier = (keys[:, None] == keys[None, :]) & (order[None, :] < order[:, None])
    slot = keys * cap + jnp.sum(earlier.astype(jnp.int32), axis=1)
    rows = jnp.arange(dest_count * cap, dtype=jnp.int32)
    return (rows[:, None] == slot[None, :]).astype(jnp.float32)


def exchange(packing, values, cap):
    sent = jnp.dot(packing, values, precision=lax.Precision.HIGHEST)
    sent = sent.reshape((sent.shape[0] // cap, cap) + values.shape[1:])
    got = lax.all_to_all(sent, "blk", split_axis=0, concat_axis=0, tiled=True)
    return got.reshape((-1,) + values.shape[1:])


def local(
    adjoint_in,
    courant,
    mixing,
    oh_rate,
    substeps,
    nest_weight,
    dest_device,
    dest_slot,
    emission_profile,
    tile_owner,
):
    blocks, lev_dev, cell_count = adjoint_in.shape
    cycle_len = nest_weight.shape[1]
    side_len = cycle_len // 4
    peer_count = lax.axis_size("blk")
    lev_groups = lax.axis_size("lev")
    my_block = lax.axis_index("blk")
    survive = jnp.exp(-oh_rate)
    cap = 2
    face_pack = pack_plan(dest_device[:, 0], peer_count, cap)
    tiles_total = blocks * peer_count // 4
    group_size = tiles_total // peer_count
    tile_pack = pack_plan(tile_owner // group_size, peer_count, cap)
    info = jnp.stack(
        [
            jnp.dot(face_pack, (dest_slot + 1).astype(jnp.float32), precision=lax.Precision.HIGHEST),
            jnp.dot(tile_pack, (tile_owner % group_size + 1).astype(jnp.float32), precision=lax.Precision.HIGHEST),
        ],
        axis=1,
    )
    info = lax.all_to_all(
        info.reshape(peer_count, cap, 2), "blk", split_axis=0, concat_axis=0, tiled=True
    ).reshape(peer_count * cap, 2)
    face_take = (
        info[:, 0][None, :] == (jnp.arange(blocks, dtype=jnp.int32) + 1).astype(jnp.float32)[:, None]
    ).astype(jnp.float32)
    tile_take = (
        info[:, 1][None, :] == (jnp.arange(group_size, dtype=jnp.int32) + 1).astype(jnp.float32)[:, None]
    ).astype(jnp.float32)
    column_mixing = lax.all_to_all(mixing, "lev", split_axis=2, concat_axis=1, tiled=True)
    adjoint = adjoint_in
    grad_sum = jnp.zeros((blocks, cell_count), jnp.float32)
    for step_index in range(STEPS):
        grad_sum = grad_sum + jnp.sum(adjoint * emission_profile[None, :, None], axis=1)
        columns = lax.all_to_all(adjoint * survive, "lev", split_axis=2, concat_axis=1, tiled=True)
        solved = solve_columns(columns, column_mixing)
        adjoint = lax.all_to_all(solved, "lev", split_axis=1, concat_axis=2, tiled=True)
        cycle_out = faces(adjoint, side_len) * nest_weight[:, None, :]
        arrived = exchange(face_pack, cycle_out.reshape(blocks, -1), cap)
        arrivals = jnp.dot(face_take, arrived, precision=lax.Precision.HIGHEST).reshape(cycle_out.shape)
        advected = adjoint
        for substep in range(RMAX):
            active = (substep < substeps)[:, None, None]
            advected = jnp.where(
                active, stencil(advected, courant[0], courant[1], side_len), advected
            )
        adjoint = add_faces(advected, arrivals, side_len)
    tile_parts = jnp.dot(tile_take, exchange(tile_pack, grad_sum, cap), precision=lax.Precision.HIGHEST)
    tile_grad = lax.psum_scatter(tile_parts, "lev", scatter_dimension=0, tiled=True)
    return (adjoint, tile_grad)


def solution(mesh):
    placed = (
        P("blk", "lev", None),
        P(None, "blk", "lev", None),
        P("blk", "lev", None),
        P("blk", "lev", None),
        P("blk"),
        P("blk", None),
        P("blk", None),
        P("blk"),
        P("lev"),
        P("blk"),
    )
    return jax.shard_map(
        local,
        mesh=mesh,
        in_specs=placed,
        out_specs=(P("blk", "lev", None), P(("blk", "lev"), None)),
        check_vma=False,
    )
```

```python
import functools

import jax
import jax.numpy as jnp
from jax import lax
from jax.experimental import pallas as pl
from jax.experimental.pallas import tpu as pltpu
from jax.sharding import PartitionSpec as P

RMAX = 4
STEPS = 2
INTERPRET = False
HI = lax.Precision.HIGHEST


def solve_kernel(ep_ref, a_ref, s_ref, k_ref, x_ref, g_ref, r_ref):
    level_count = a_ref.shape[0]
    grad = ep_ref[0] * a_ref[0]
    for level in range(1, level_count):
        grad = grad + ep_ref[level] * a_ref[level]
    g_ref[...] = grad
    prev_ratio = None
    prev_scaled = None
    for level in range(level_count):
        right = a_ref[level] * s_ref[level]
        lower_k = k_ref[level - 1] if level > 0 else None
        upper_k = k_ref[level] if level < level_count - 1 else None
        if level == 0:
            pivot_val = 1.0 + upper_k
            scaled = right / pivot_val
        else:
            diag_term = 1.0 + lower_k if upper_k is None else 1.0 + lower_k + upper_k
            pivot_val = diag_term + lower_k * prev_ratio
            scaled = (right + lower_k * prev_scaled) / pivot_val
        x_ref[level] = scaled
        if upper_k is not None:
            prev_ratio = -upper_k / pivot_val
            r_ref[level] = prev_ratio
        prev_scaled = scaled
    solved = prev_scaled
    for level in range(level_count - 2, -1, -1):
        solved = x_ref[level] - r_ref[level] * solved
        x_ref[level] = solved


def column_solve(ep, adjoint, survive, mixing):
    level_count, blocks, cells = adjoint.shape
    chunk = 256
    spec = pl.BlockSpec((level_count, blocks, chunk), lambda c: (0, 0, c))
    return pl.pallas_call(
        solve_kernel,
        grid=(cells // chunk,),
        in_specs=[pl.BlockSpec(memory_space=pltpu.SMEM), spec, spec, spec],
        out_specs=[spec, pl.BlockSpec((blocks, chunk), lambda c: (0, c))],
        out_shape=[
            jax.ShapeDtypeStruct(adjoint.shape, jnp.float32),
            jax.ShapeDtypeStruct((blocks, cells), jnp.float32),
        ],
        scratch_shapes=[pltpu.VMEM((level_count, blocks, chunk), jnp.float32)],
        interpret=INTERPRET,
    )(ep, adjoint, survive, mixing)


def stencil_kernel(side_len, st_ref, v_ref, e_ref, n_ref, add_ref, o_ref):
    v = v_ref[...]
    east_c = e_ref[...]
    north_c = n_ref[...]
    cells = v.shape[1]
    lane = lax.broadcasted_iota(jnp.int32, v.shape, 1)
    east_ok = lane % side_len != side_len - 1
    north_ok = lane < cells - side_len
    keep = 1.0 - east_c - north_c
    steps = st_ref[...]
    for substep in range(RMAX):
        east_adj = jnp.where(east_ok, pltpu.roll(v, cells - 1, 1), 0.0)
        north_adj = jnp.where(north_ok, pltpu.roll(v, cells - side_len, 1), 0.0)
        moved = keep * v + east_c * east_adj + north_c * north_adj
        v = jnp.where(substep < steps, moved, v)
    o_ref[...] = v + add_ref[...]


def advect(side_len, steps, adjoint, east_c, north_c, added):
    rows, cells = adjoint.shape
    tile = 64
    spec = pl.BlockSpec((tile, cells), lambda r: (r, 0))
    return pl.pallas_call(
        functools.partial(stencil_kernel, side_len),
        grid=(rows // tile,),
        in_specs=[pl.BlockSpec((tile, 1), lambda r: (r, 0)), spec, spec, spec, spec],
        out_specs=spec,
        out_shape=jax.ShapeDtypeStruct(adjoint.shape, jnp.float32),
        interpret=INTERPRET,
    )(steps, adjoint, east_c, north_c, added)


def face_matrix(side_len, cells):
    pos = jnp.arange(side_len, dtype=jnp.int32)
    where = jnp.concatenate([pos, (side_len - 1) * side_len + pos, pos * side_len, pos * side_len + side_len - 1])
    return (jnp.arange(cells, dtype=jnp.int32)[:, None] == where[None, :]).astype(jnp.float32)


def pack_plan(keys, dest_count, cap):
    count = keys.shape[0]
    order = jnp.arange(count, dtype=jnp.int32)
    earlier = (keys[:, None] == keys[None, :]) & (order[None, :] < order[:, None])
    slot = keys * cap + jnp.sum(earlier.astype(jnp.int32), axis=1)
    rows = jnp.arange(dest_count * cap, dtype=jnp.int32)
    return (rows[:, None] == slot[None, :]).astype(jnp.float32)


def to_columns(x):
    return lax.all_to_all(x, "lev", split_axis=x.ndim - 2, concat_axis=x.ndim - 3, tiled=True)


def local(
    adjoint_in,
    courant,
    mixing,
    oh_rate,
    substeps,
    nest_weight,
    dest_device,
    dest_slot,
    emission_profile,
    tile_owner,
):
    blocks, lev_dev, cell_count = adjoint_in.shape
    cycle_len = nest_weight.shape[1]
    side_len = cycle_len // 4
    peer_count = lax.axis_size("blk")
    lev_groups = lax.axis_size("lev")
    lev_index = lax.axis_index("lev")
    own = blocks // lev_groups
    levels = lev_dev * lev_groups
    cap = 2

    state = to_columns(jnp.stack([adjoint_in, jnp.exp(-oh_rate), mixing]).transpose(0, 2, 1, 3))
    adjoint, survive, column_mixing = state[0], state[1], state[2]
    flows = to_columns(courant.transpose(0, 2, 1, 3)).reshape(2, levels * own, cell_count)
    ep = jnp.broadcast_to(emission_profile[:, None], (lev_dev, lev_groups))
    ep = lax.all_to_all(ep, "lev", split_axis=1, concat_axis=0, tiled=True).reshape(levels)

    own_steps = lax.dynamic_slice_in_dim(substeps, lev_index * own, own)
    row_steps = jnp.tile(own_steps, levels)[:, None]
    own_weight = lax.dynamic_slice_in_dim(nest_weight, lev_index * own, own)
    own_owner = lax.dynamic_slice_in_dim(tile_owner, lev_index * own, own)

    face_pack = pack_plan(dest_device[:, 0], peer_count, cap)
    tiles_total = blocks * peer_count // 4
    group_size = tiles_total // peer_count
    tile_pack = pack_plan(own_owner // group_size, peer_count, cap)
    info = jnp.stack(
        [
            jnp.dot(face_pack, (dest_slot + 1).astype(jnp.float32), precision=HI),
            jnp.dot(tile_pack, (own_owner % group_size + 1).astype(jnp.float32), precision=HI),
        ],
        axis=1,
    )
    info = lax.all_to_all(
        info.reshape(peer_count, cap, 2), "blk", split_axis=0, concat_axis=0, tiled=True
    ).reshape(peer_count * cap, 2)
    face_take = (
        info[:, 0][None, :] == (jnp.arange(blocks, dtype=jnp.int32) + 1).astype(jnp.float32)[:, None]
    ).astype(jnp.float32)
    tile_take = (
        info[:, 1][None, :] == (jnp.arange(group_size, dtype=jnp.int32) + 1).astype(jnp.float32)[:, None]
    ).astype(jnp.float32)

    pick = face_matrix(side_len, cell_count)
    grad_sum = jnp.zeros((own, cell_count), jnp.float32)
    for step_index in range(STEPS):
        solved, grad_step = column_solve(ep, adjoint, survive, column_mixing)
        grad_sum = grad_sum + grad_step
        flat = solved.reshape(levels * own, cell_count)
        cycle_out = jnp.dot(flat, pick, precision=HI).reshape(levels, own, cycle_len) * own_weight[None]
        by_level = lax.all_to_all(cycle_out, "lev", split_axis=0, concat_axis=1, tiled=True)
        sent = jnp.einsum("sb,lbk->slk", face_pack, by_level, precision=HI)
        sent = sent.reshape(peer_count, cap, lev_dev, cycle_len)
        got = lax.all_to_all(sent, "blk", split_axis=0, concat_axis=0, tiled=True)
        got = got.reshape(peer_count * cap, lev_dev, cycle_len)
        arrivals = jnp.einsum("ts,slk->ltk", face_take, got, precision=HI)
        arrivals = to_columns(arrivals).reshape(levels * own, cycle_len)
        added = jnp.dot(arrivals, pick.T, precision=HI)
        adjoint = advect(side_len, row_steps, flat, flows[0], flows[1], added).reshape(levels, own, cell_count)

    tile_sent = jnp.dot(tile_pack, grad_sum, precision=HI).reshape(peer_count, cap, cell_count)
    tile_got = lax.all_to_all(tile_sent, "blk", split_axis=0, concat_axis=0, tiled=True)
    tile_parts = jnp.dot(tile_take, tile_got.reshape(peer_count * cap, cell_count), precision=HI)
    tile_parts = lax.all_to_all(
        tile_parts.reshape(lev_groups, group_size // lev_groups, cell_count),
        "lev",
        split_axis=0,
        concat_axis=0,
        tiled=True,
    )
    tile_grad = jnp.sum(tile_parts, axis=0)
    adjoint_out = lax.all_to_all(adjoint, "lev", split_axis=0, concat_axis=1, tiled=True)
    return (adjoint_out.transpose(1, 0, 2), tile_grad)


def solution(mesh):
    placed = (
        P("blk", "lev", None),
        P(None, "blk", "lev", None),
        P("blk", "lev", None),
        P("blk", "lev", None),
        P("blk"),
        P("blk", None),
        P("blk", None),
        P("blk"),
        P("lev"),
        P("blk"),
    )
    return jax.shard_map(
        local,
        mesh=mesh,
        in_specs=placed,
        out_specs=(P("blk", "lev", None), P(("blk", "lev"), None)),
        check_vma=False,
    )
```

```python
import functools

import jax
import jax.numpy as jnp
from jax import lax
from jax.experimental import pallas as pl
from jax.experimental.pallas import tpu as pltpu
from jax.sharding import PartitionSpec as P

RMAX = 4
STEPS = 2
INTERPRET = False
HI = lax.Precision.HIGHEST


def solve_kernel(ep_ref, a_ref, s_ref, k_ref, x_ref, g_ref, r_ref):
    level_count = a_ref.shape[0]
    grad = ep_ref[0] * a_ref[0]
    for level in range(1, level_count):
        grad = grad + ep_ref[level] * a_ref[level]
    g_ref[...] = grad
    prev_ratio = None
    prev_scaled = None
    for level in range(level_count):
        right = a_ref[level] * s_ref[level]
        lower_k = k_ref[level - 1] if level > 0 else None
        upper_k = k_ref[level] if level < level_count - 1 else None
        if level == 0:
            pivot_val = 1.0 + upper_k
            scaled = right / pivot_val
        else:
            diag_term = 1.0 + lower_k if upper_k is None else 1.0 + lower_k + upper_k
            pivot_val = diag_term + lower_k * prev_ratio
            scaled = (right + lower_k * prev_scaled) / pivot_val
        x_ref[level] = scaled
        if upper_k is not None:
            prev_ratio = -upper_k / pivot_val
            r_ref[level] = prev_ratio
        prev_scaled = scaled
    solved = prev_scaled
    for level in range(level_count - 2, -1, -1):
        solved = x_ref[level] - r_ref[level] * solved
        x_ref[level] = solved


def column_solve(ep, adjoint, survive, mixing):
    level_count, blocks, cells = adjoint.shape
    chunk = 256
    spec = pl.BlockSpec((level_count, blocks, chunk), lambda c: (0, 0, c))
    return pl.pallas_call(
        solve_kernel,
        grid=(cells // chunk,),
        in_specs=[pl.BlockSpec(memory_space=pltpu.SMEM), spec, spec, spec],
        out_specs=[spec, pl.BlockSpec((blocks, chunk), lambda c: (0, c))],
        out_shape=[
            jax.ShapeDtypeStruct(adjoint.shape, jnp.float32),
            jax.ShapeDtypeStruct((blocks, cells), jnp.float32),
        ],
        scratch_shapes=[pltpu.VMEM((level_count, blocks, chunk), jnp.float32)],
        interpret=INTERPRET,
    )(ep, adjoint, survive, mixing)


def stencil_kernel(side_len, st_ref, v_ref, e_ref, n_ref, add_ref, o_ref):
    v = v_ref[...]
    east_c = e_ref[...]
    north_c = n_ref[...]
    cells = v.shape[1]
    lane = lax.broadcasted_iota(jnp.int32, v.shape, 1)
    east_ok = lane % side_len != side_len - 1
    north_ok = lane < cells - side_len
    keep = 1.0 - east_c - north_c
    steps = st_ref[...]
    for substep in range(RMAX):
        east_adj = jnp.where(east_ok, pltpu.roll(v, cells - 1, 1), 0.0)
        north_adj = jnp.where(north_ok, pltpu.roll(v, cells - side_len, 1), 0.0)
        moved = keep * v + east_c * east_adj + north_c * north_adj
        v = jnp.where(substep < steps, moved, v)
    o_ref[...] = v + add_ref[...]


def advect(side_len, steps, adjoint, east_c, north_c, added):
    rows, cells = adjoint.shape
    tile = 64
    spec = pl.BlockSpec((tile, cells), lambda r: (r, 0))
    return pl.pallas_call(
        functools.partial(stencil_kernel, side_len),
        grid=(rows // tile,),
        in_specs=[pl.BlockSpec((tile, 1), lambda r: (r, 0)), spec, spec, spec, spec],
        out_specs=spec,
        out_shape=jax.ShapeDtypeStruct(adjoint.shape, jnp.float32),
        interpret=INTERPRET,
    )(steps, adjoint, east_c, north_c, added)


def face_matrix(side_len, cells):
    pos = jnp.arange(side_len, dtype=jnp.int32)
    where = jnp.concatenate([pos, (side_len - 1) * side_len + pos, pos * side_len, pos * side_len + side_len - 1])
    return (jnp.arange(cells, dtype=jnp.int32)[:, None] == where[None, :]).astype(jnp.float32)


def pack_plan(keys, dest_count, cap):
    count = keys.shape[0]
    order = jnp.arange(count, dtype=jnp.int32)
    earlier = (keys[:, None] == keys[None, :]) & (order[None, :] < order[:, None])
    slot = keys * cap + jnp.sum(earlier.astype(jnp.int32), axis=1)
    rows = jnp.arange(dest_count * cap, dtype=jnp.int32)
    return (rows[:, None] == slot[None, :]).astype(jnp.float32)


def to_columns(x):
    return lax.all_to_all(x, "lev", split_axis=x.ndim - 2, concat_axis=x.ndim - 3, tiled=True)


def local(
    adjoint_in,
    courant,
    mixing,
    oh_rate,
    substeps,
    nest_weight,
    dest_device,
    dest_slot,
    emission_profile,
    tile_owner,
):
    blocks, lev_dev, cell_count = adjoint_in.shape
    cycle_len = nest_weight.shape[1]
    side_len = cycle_len // 4
    peer_count = lax.axis_size("blk")
    lev_groups = lax.axis_size("lev")
    lev_index = lax.axis_index("lev")
    own = blocks // lev_groups
    levels = lev_dev * lev_groups
    cap = 2

    state = to_columns(jnp.stack([adjoint_in, jnp.exp(-oh_rate), mixing]).transpose(0, 2, 1, 3))
    adjoint, survive, column_mixing = state[0], state[1], state[2]
    flows = to_columns(courant.transpose(0, 2, 1, 3)).reshape(2, levels * own, cell_count)
    ep = jnp.broadcast_to(emission_profile[:, None], (lev_dev, lev_groups))
    ep = lax.all_to_all(ep, "lev", split_axis=1, concat_axis=0, tiled=True).reshape(levels)

    own_steps = lax.dynamic_slice_in_dim(substeps, lev_index * own, own)
    row_steps = jnp.tile(own_steps, levels)[:, None]
    own_weight = lax.dynamic_slice_in_dim(nest_weight, lev_index * own, own)
    own_owner = lax.dynamic_slice_in_dim(tile_owner, lev_index * own, own)

    face_pack = pack_plan(dest_device[:, 0], peer_count, cap)
    tiles_total = blocks * peer_count // 4
    group_size = tiles_total // peer_count
    tile_pack = pack_plan(own_owner // group_size, peer_count, cap)
    info = jnp.stack(
        [
            jnp.dot(face_pack, (dest_slot + 1).astype(jnp.float32), precision=HI),
            jnp.dot(tile_pack, (own_owner % group_size + 1).astype(jnp.float32), precision=HI),
        ],
        axis=1,
    )
    info = jnp.pad(info, ((0, 0), (0, cycle_len - 2))).reshape(peer_count, cap, cycle_len)
    face_width = lev_dev * cycle_len

    pick = face_matrix(side_len, cell_count)
    grad_sum = jnp.zeros((own, cell_count), jnp.float32)
    for step_index in range(STEPS):
        solved, grad_step = column_solve(ep, adjoint, survive, column_mixing)
        grad_sum = grad_sum + grad_step
        flat = solved.reshape(levels * own, cell_count)
        cycle_out = jnp.dot(flat, pick, precision=HI).reshape(levels, own, cycle_len) * own_weight[None]
        by_level = lax.all_to_all(cycle_out, "lev", split_axis=0, concat_axis=1, tiled=True)
        sent = jnp.einsum("sb,lbk->slk", face_pack, by_level, precision=HI)
        sent = sent.reshape(peer_count, cap, face_width)
        if step_index == 0:
            sent = jnp.concatenate([sent, info], axis=2)
        if step_index == STEPS - 1:
            tile_sent = jnp.dot(tile_pack, grad_sum, precision=HI).reshape(peer_count, cap, cell_count)
            sent = jnp.concatenate([sent, tile_sent], axis=2)
        got = lax.all_to_all(sent, "blk", split_axis=0, concat_axis=0, tiled=True)
        got = got.reshape(peer_count * cap, -1)
        if step_index == 0:
            face_take = (
                got[:, face_width][None, :]
                == (jnp.arange(blocks, dtype=jnp.int32) + 1).astype(jnp.float32)[:, None]
            ).astype(jnp.float32)
            tile_take = (
                got[:, face_width + 1][None, :]
                == (jnp.arange(group_size, dtype=jnp.int32) + 1).astype(jnp.float32)[:, None]
            ).astype(jnp.float32)
        if step_index == STEPS - 1:
            tile_got = got[:, face_width:]
        got = got[:, :face_width].reshape(peer_count * cap, lev_dev, cycle_len)
        arrivals = jnp.einsum("ts,slk->ltk", face_take, got, precision=HI)
        arrivals = to_columns(arrivals).reshape(levels * own, cycle_len)
        added = jnp.dot(arrivals, pick.T, precision=HI)
        adjoint = advect(side_len, row_steps, flat, flows[0], flows[1], added).reshape(levels, own, cell_count)

    tile_parts = jnp.dot(tile_take, tile_got, precision=HI)
    tile_rows = group_size // lev_groups
    packed = jnp.concatenate(
        [
            adjoint.reshape(lev_groups, lev_dev * own, cell_count),
            tile_parts.reshape(lev_groups, tile_rows, cell_count),
        ],
        axis=1,
    )
    packed = lax.all_to_all(packed, "lev", split_axis=0, concat_axis=0, tiled=True)
    tile_grad = jnp.sum(packed[:, lev_dev * own :], axis=0)
    adjoint_out = packed[:, : lev_dev * own].reshape(lev_groups, lev_dev, own, cell_count)
    adjoint_out = adjoint_out.transpose(0, 2, 1, 3).reshape(blocks, lev_dev, cell_count)
    return (adjoint_out, tile_grad)


def solution(mesh):
    placed = (
        P("blk", "lev", None),
        P(None, "blk", "lev", None),
        P("blk", "lev", None),
        P("blk", "lev", None),
        P("blk"),
        P("blk", None),
        P("blk", None),
        P("blk"),
        P("lev"),
        P("blk"),
    )
    return jax.shard_map(
        local,
        mesh=mesh,
        in_specs=placed,
        out_specs=(P("blk", "lev", None), P(("blk", "lev"), None)),
        check_vma=False,
    )
```

```python
import functools

import jax
import jax.numpy as jnp
from jax import lax
from jax.experimental import pallas as pl
from jax.experimental.pallas import tpu as pltpu
from jax.sharding import PartitionSpec as P

RMAX = 4
STEPS = 2
INTERPRET = False
HI = lax.Precision.HIGHEST


def solve_kernel(ep_ref, a_ref, s_ref, k_ref, x_ref, g_ref, r_ref):
    level_count = a_ref.shape[0]
    grad = ep_ref[0] * a_ref[0]
    for level in range(1, level_count):
        grad = grad + ep_ref[level] * a_ref[level]
    g_ref[...] = grad
    prev_ratio = None
    prev_scaled = None
    for level in range(level_count):
        right = a_ref[level] * s_ref[level]
        lower_k = k_ref[level - 1] if level > 0 else None
        upper_k = k_ref[level] if level < level_count - 1 else None
        if level == 0:
            pivot_val = 1.0 + upper_k
            scaled = right / pivot_val
        else:
            diag_term = 1.0 + lower_k if upper_k is None else 1.0 + lower_k + upper_k
            pivot_val = diag_term + lower_k * prev_ratio
            scaled = (right + lower_k * prev_scaled) / pivot_val
        x_ref[level] = scaled
        if upper_k is not None:
            prev_ratio = -upper_k / pivot_val
            r_ref[level] = prev_ratio
        prev_scaled = scaled
    solved = prev_scaled
    for level in range(level_count - 2, -1, -1):
        solved = x_ref[level] - r_ref[level] * solved
        x_ref[level] = solved


def column_solve(ep, adjoint, survive, mixing):
    level_count, blocks, cells = adjoint.shape
    chunk = 256
    spec = pl.BlockSpec((level_count, blocks, chunk), lambda c: (0, 0, c))
    return pl.pallas_call(
        solve_kernel,
        grid=(cells // chunk,),
        in_specs=[pl.BlockSpec(memory_space=pltpu.SMEM), spec, spec, spec],
        out_specs=[spec, pl.BlockSpec((blocks, chunk), lambda c: (0, c))],
        out_shape=[
            jax.ShapeDtypeStruct(adjoint.shape, jnp.float32),
            jax.ShapeDtypeStruct((blocks, cells), jnp.float32),
        ],
        scratch_shapes=[pltpu.VMEM((level_count, blocks, chunk), jnp.float32)],
        interpret=INTERPRET,
    )(ep, adjoint, survive, mixing)


def stencil_kernel(side_len, st_ref, v_ref, e_ref, n_ref, add_ref, o_ref):
    v = v_ref[...]
    east_c = e_ref[...]
    north_c = n_ref[...]
    cells = v.shape[1]
    lane = lax.broadcasted_iota(jnp.int32, v.shape, 1)
    east_ok = lane % side_len != side_len - 1
    north_ok = lane < cells - side_len
    keep = 1.0 - east_c - north_c
    steps = st_ref[...]
    for substep in range(RMAX):
        east_adj = jnp.where(east_ok, pltpu.roll(v, cells - 1, 1), 0.0)
        north_adj = jnp.where(north_ok, pltpu.roll(v, cells - side_len, 1), 0.0)
        moved = keep * v + east_c * east_adj + north_c * north_adj
        v = jnp.where(substep < steps, moved, v)
    o_ref[...] = v + add_ref[...]


def advect(side_len, steps, adjoint, east_c, north_c, added):
    rows, cells = adjoint.shape
    tile = 64
    spec = pl.BlockSpec((tile, cells), lambda r: (r, 0))
    return pl.pallas_call(
        functools.partial(stencil_kernel, side_len),
        grid=(rows // tile,),
        in_specs=[pl.BlockSpec((tile, 1), lambda r: (r, 0)), spec, spec, spec, spec],
        out_specs=spec,
        out_shape=jax.ShapeDtypeStruct(adjoint.shape, jnp.float32),
        interpret=INTERPRET,
    )(steps, adjoint, east_c, north_c, added)


def face_matrix(side_len, cells):
    pos = jnp.arange(side_len, dtype=jnp.int32)
    where = jnp.concatenate([pos, (side_len - 1) * side_len + pos, pos * side_len, pos * side_len + side_len - 1])
    return (jnp.arange(cells, dtype=jnp.int32)[:, None] == where[None, :]).astype(jnp.float32)


def pack_plan(keys, dest_count, cap):
    count = keys.shape[0]
    order = jnp.arange(count, dtype=jnp.int32)
    earlier = (keys[:, None] == keys[None, :]) & (order[None, :] < order[:, None])
    slot = keys * cap + jnp.sum(earlier.astype(jnp.int32), axis=1)
    rows = jnp.arange(dest_count * cap, dtype=jnp.int32)
    return (rows[:, None] == slot[None, :]).astype(jnp.float32)


def to_columns(x):
    return lax.all_to_all(x, "lev", split_axis=x.ndim - 2, concat_axis=x.ndim - 3, tiled=True)


def ring_columns(x, lev_index, lev_groups):
    lead = x.shape[:-3]
    lev_dev, blocks, cells = x.shape[-3:]
    own = blocks // lev_groups
    parts = x.reshape(lead + (lev_dev, lev_groups, own, cells))
    got = []
    for shift in range(lev_groups):
        piece = lax.dynamic_index_in_dim(parts, (lev_index + shift) % lev_groups, axis=len(lead) + 1, keepdims=False)
        if shift:
            ring = [(src, (src + shift) % lev_groups) for src in range(lev_groups)]
            piece = lax.ppermute(piece, "lev", ring)
        got.append(piece)
    got = jnp.stack(got, axis=len(lead))
    order = (lev_index - jnp.arange(lev_groups, dtype=jnp.int32)) % lev_groups
    got = jnp.take(got, order, axis=len(lead))
    return got.reshape(lead + (lev_groups * lev_dev, own, cells))


def local(
    adjoint_in,
    courant,
    mixing,
    oh_rate,
    substeps,
    nest_weight,
    dest_device,
    dest_slot,
    emission_profile,
    tile_owner,
):
    blocks, lev_dev, cell_count = adjoint_in.shape
    cycle_len = nest_weight.shape[1]
    side_len = cycle_len // 4
    peer_count = lax.axis_size("blk")
    lev_groups = lax.axis_size("lev")
    lev_index = lax.axis_index("lev")
    own = blocks // lev_groups
    levels = lev_dev * lev_groups
    cap = 2

    state = to_columns(jnp.stack([adjoint_in, jnp.exp(-oh_rate), mixing]).transpose(0, 2, 1, 3))
    adjoint, survive, column_mixing = state[0], state[1], state[2]
    flows = courant.transpose(0, 2, 1, 3)
    ep = jnp.broadcast_to(emission_profile[:, None], (lev_dev, lev_groups))
    ep = lax.all_to_all(ep, "lev", split_axis=1, concat_axis=0, tiled=True).reshape(levels)

    own_steps = lax.dynamic_slice_in_dim(substeps, lev_index * own, own)
    row_steps = jnp.tile(own_steps, levels)[:, None]
    own_weight = lax.dynamic_slice_in_dim(nest_weight, lev_index * own, own)
    own_owner = lax.dynamic_slice_in_dim(tile_owner, lev_index * own, own)

    face_pack = pack_plan(dest_device[:, 0], peer_count, cap)
    tiles_total = blocks * peer_count // 4
    group_size = tiles_total // peer_count
    tile_pack = pack_plan(own_owner // group_size, peer_count, cap)
    info = jnp.stack(
        [
            jnp.dot(face_pack, (dest_slot + 1).astype(jnp.float32), precision=HI),
            jnp.dot(tile_pack, (own_owner % group_size + 1).astype(jnp.float32), precision=HI),
        ],
        axis=1,
    )
    info = jnp.pad(info, ((0, 0), (0, cycle_len - 2))).reshape(peer_count, cap, cycle_len)
    face_width = lev_dev * cycle_len

    pick = face_matrix(side_len, cell_count)
    grad_sum = jnp.zeros((own, cell_count), jnp.float32)
    for step_index in range(STEPS):
        solved, grad_step = column_solve(ep, adjoint, survive, column_mixing)
        if step_index == 0:
            flows, solved = lax.optimization_barrier((flows, solved))
            flows = ring_columns(flows, lev_index, lev_groups).reshape(2, levels * own, cell_count)
        grad_sum = grad_sum + grad_step
        flat = solved.reshape(levels * own, cell_count)
        cycle_out = jnp.dot(flat, pick, precision=HI).reshape(levels, own, cycle_len) * own_weight[None]
        by_level = lax.all_to_all(cycle_out, "lev", split_axis=0, concat_axis=1, tiled=True)
        sent = jnp.einsum("sb,lbk->slk", face_pack, by_level, precision=HI)
        sent = sent.reshape(peer_count, cap, face_width)
        if step_index == 0:
            sent = jnp.concatenate([sent, info], axis=2)
        if step_index == STEPS - 1:
            tile_sent = jnp.dot(tile_pack, grad_sum, precision=HI).reshape(peer_count, cap, cell_count)
            sent = jnp.concatenate([sent, tile_sent], axis=2)
        got = lax.all_to_all(sent, "blk", split_axis=0, concat_axis=0, tiled=True)
        got = got.reshape(peer_count * cap, -1)
        if step_index == 0:
            face_take = (
                got[:, face_width][None, :]
                == (jnp.arange(blocks, dtype=jnp.int32) + 1).astype(jnp.float32)[:, None]
            ).astype(jnp.float32)
            tile_take = (
                got[:, face_width + 1][None, :]
                == (jnp.arange(group_size, dtype=jnp.int32) + 1).astype(jnp.float32)[:, None]
            ).astype(jnp.float32)
        if step_index == STEPS - 1:
            tile_got = got[:, face_width:]
        got = got[:, :face_width].reshape(peer_count * cap, lev_dev, cycle_len)
        arrivals = jnp.einsum("ts,slk->ltk", face_take, got, precision=HI)
        arrivals = to_columns(arrivals).reshape(levels * own, cycle_len)
        added = jnp.dot(arrivals, pick.T, precision=HI)
        adjoint = advect(side_len, row_steps, flat, flows[0], flows[1], added).reshape(levels, own, cell_count)

    tile_parts = jnp.dot(tile_take, tile_got, precision=HI)
    tile_rows = group_size // lev_groups
    packed = jnp.concatenate(
        [
            adjoint.reshape(lev_groups, lev_dev * own, cell_count),
            tile_parts.reshape(lev_groups, tile_rows, cell_count),
        ],
        axis=1,
    )
    packed = lax.all_to_all(packed, "lev", split_axis=0, concat_axis=0, tiled=True)
    tile_grad = jnp.sum(packed[:, lev_dev * own :], axis=0)
    adjoint_out = packed[:, : lev_dev * own].reshape(lev_groups, lev_dev, own, cell_count)
    adjoint_out = adjoint_out.transpose(0, 2, 1, 3).reshape(blocks, lev_dev, cell_count)
    return (adjoint_out, tile_grad)


def solution(mesh):
    placed = (
        P("blk", "lev", None),
        P(None, "blk", "lev", None),
        P("blk", "lev", None),
        P("blk", "lev", None),
        P("blk"),
        P("blk", None),
        P("blk", None),
        P("blk"),
        P("lev"),
        P("blk"),
    )
    return jax.shard_map(
        local,
        mesh=mesh,
        in_specs=placed,
        out_specs=(P("blk", "lev", None), P(("blk", "lev"), None)),
        check_vma=False,
    )
```

```python
import functools

import jax
import jax.numpy as jnp
from jax import lax
from jax.experimental import pallas as pl
from jax.experimental.pallas import tpu as pltpu
from jax.sharding import PartitionSpec as P

RMAX = 4
STEPS = 2
INTERPRET = False
HI = lax.Precision.HIGHEST


def eliminate(right_of, k_ref, x_ref, r_ref):
    level_count = k_ref.shape[0]
    prev_ratio = None
    prev_scaled = None
    for level in range(level_count):
        right = right_of(level)
        lower_k = k_ref[level - 1] if level > 0 else None
        upper_k = k_ref[level] if level < level_count - 1 else None
        if level == 0:
            pivot_val = 1.0 + upper_k
            scaled = right / pivot_val
        else:
            diag_term = 1.0 + lower_k if upper_k is None else 1.0 + lower_k + upper_k
            pivot_val = diag_term + lower_k * prev_ratio
            scaled = (right + lower_k * prev_scaled) / pivot_val
        x_ref[level] = scaled
        if upper_k is not None:
            prev_ratio = -upper_k / pivot_val
            r_ref[level] = prev_ratio
        prev_scaled = scaled
    solved = prev_scaled
    for level in range(level_count - 2, -1, -1):
        solved = x_ref[level] - r_ref[level] * solved
        x_ref[level] = solved


def first_kernel(b_ref, k_ref, x_ref, r_ref):
    eliminate(lambda level: b_ref[level], k_ref, x_ref, r_ref)


def next_kernel(ep_ref, a_ref, s_ref, k_ref, x_ref, g_ref, r_ref):
    level_count = a_ref.shape[0]
    grad = ep_ref[0] * a_ref[0]
    for level in range(1, level_count):
        grad = grad + ep_ref[level] * a_ref[level]
    g_ref[...] = grad
    eliminate(lambda level: a_ref[level] * s_ref[level], k_ref, x_ref, r_ref)


def column_solve(mixing, right=None, ep=None, adjoint=None, survive=None):
    level_count, blocks, cells = mixing.shape
    chunk = 256
    spec = pl.BlockSpec((level_count, blocks, chunk), lambda c: (0, 0, c))
    scratch = [pltpu.VMEM((level_count, blocks, chunk), jnp.float32)]
    solved_shape = jax.ShapeDtypeStruct(mixing.shape, jnp.float32)
    if right is not None:
        return pl.pallas_call(
            first_kernel,
            grid=(cells // chunk,),
            in_specs=[spec, spec],
            out_specs=spec,
            out_shape=solved_shape,
            scratch_shapes=scratch,
            interpret=INTERPRET,
        )(right, mixing)
    return pl.pallas_call(
        next_kernel,
        grid=(cells // chunk,),
        in_specs=[pl.BlockSpec(memory_space=pltpu.SMEM), spec, spec, spec],
        out_specs=[spec, pl.BlockSpec((blocks, chunk), lambda c: (0, c))],
        out_shape=[solved_shape, jax.ShapeDtypeStruct((blocks, cells), jnp.float32)],
        scratch_shapes=scratch,
        interpret=INTERPRET,
    )(ep, adjoint, survive, mixing)


def stencil_kernel(side_len, st_ref, v_ref, e_ref, n_ref, add_ref, o_ref):
    v = v_ref[...]
    east_c = e_ref[...]
    north_c = n_ref[...]
    cells = v.shape[1]
    lane = lax.broadcasted_iota(jnp.int32, v.shape, 1)
    east_ok = lane % side_len != side_len - 1
    north_ok = lane < cells - side_len
    keep = 1.0 - east_c - north_c
    steps = st_ref[...]
    for substep in range(RMAX):
        east_adj = jnp.where(east_ok, pltpu.roll(v, cells - 1, 1), 0.0)
        north_adj = jnp.where(north_ok, pltpu.roll(v, cells - side_len, 1), 0.0)
        moved = keep * v + east_c * east_adj + north_c * north_adj
        v = jnp.where(substep < steps, moved, v)
    o_ref[...] = v + add_ref[...]


def advect(side_len, steps, adjoint, east_c, north_c, added):
    rows, cells = adjoint.shape
    tile = 64
    spec = pl.BlockSpec((tile, cells), lambda r: (r, 0))
    return pl.pallas_call(
        functools.partial(stencil_kernel, side_len),
        grid=(rows // tile,),
        in_specs=[pl.BlockSpec((tile, 1), lambda r: (r, 0)), spec, spec, spec, spec],
        out_specs=spec,
        out_shape=jax.ShapeDtypeStruct(adjoint.shape, jnp.float32),
        interpret=INTERPRET,
    )(steps, adjoint, east_c, north_c, added)


def face_matrix(side_len, cells):
    pos = jnp.arange(side_len, dtype=jnp.int32)
    where = jnp.concatenate([pos, (side_len - 1) * side_len + pos, pos * side_len, pos * side_len + side_len - 1])
    return (jnp.arange(cells, dtype=jnp.int32)[:, None] == where[None, :]).astype(jnp.float32)


def pack_plan(keys, dest_count, cap):
    count = keys.shape[0]
    order = jnp.arange(count, dtype=jnp.int32)
    earlier = (keys[:, None] == keys[None, :]) & (order[None, :] < order[:, None])
    slot = keys * cap + jnp.sum(earlier.astype(jnp.int32), axis=1)
    rows = jnp.arange(dest_count * cap, dtype=jnp.int32)
    return (rows[:, None] == slot[None, :]).astype(jnp.float32)


def to_columns(x):
    return lax.all_to_all(x, "lev", split_axis=x.ndim - 2, concat_axis=x.ndim - 3, tiled=True)


def ring_columns(x, lev_index, lev_groups):
    lead = x.shape[:-3]
    lev_dev, blocks, cells = x.shape[-3:]
    own = blocks // lev_groups
    parts = x.reshape(lead + (lev_dev, lev_groups, own, cells))
    got = []
    for shift in range(lev_groups):
        piece = lax.dynamic_index_in_dim(parts, (lev_index + shift) % lev_groups, axis=len(lead) + 1, keepdims=False)
        if shift:
            ring = [(src, (src + shift) % lev_groups) for src in range(lev_groups)]
            piece = lax.ppermute(piece, "lev", ring)
        got.append(piece)
    got = jnp.stack(got, axis=len(lead))
    order = (lev_index - jnp.arange(lev_groups, dtype=jnp.int32)) % lev_groups
    got = jnp.take(got, order, axis=len(lead))
    return got.reshape(lead + (lev_groups * lev_dev, own, cells))


def local(
    adjoint_in,
    courant,
    mixing,
    oh_rate,
    substeps,
    nest_weight,
    dest_device,
    dest_slot,
    emission_profile,
    tile_owner,
):
    blocks, lev_dev, cell_count = adjoint_in.shape
    cycle_len = nest_weight.shape[1]
    side_len = cycle_len // 4
    peer_count = lax.axis_size("blk")
    lev_groups = lax.axis_size("lev")
    lev_index = lax.axis_index("lev")
    own = blocks // lev_groups
    levels = lev_dev * lev_groups
    cap = 2

    survive = jnp.exp(-oh_rate)
    state = to_columns(jnp.stack([adjoint_in * survive, mixing]).transpose(0, 2, 1, 3))
    right, column_mixing = state[0], state[1]
    ep = jnp.broadcast_to(emission_profile[:, None, None], (lev_dev, lev_groups, 1))
    deferred = (courant.transpose(0, 2, 1, 3), survive.transpose(1, 0, 2), ep)
    grad_sum = jnp.sum(adjoint_in * emission_profile[None, :, None], axis=1)

    own_steps = lax.dynamic_slice_in_dim(substeps, lev_index * own, own)
    row_steps = jnp.tile(own_steps, levels)[:, None]
    own_weight = lax.dynamic_slice_in_dim(nest_weight, lev_index * own, own)

    face_pack = pack_plan(dest_device[:, 0], peer_count, cap)
    tiles_total = blocks * peer_count // 4
    group_size = tiles_total // peer_count
    tile_pack = pack_plan(tile_owner // group_size, peer_count, cap)
    info = jnp.stack(
        [
            jnp.dot(face_pack, (dest_slot + 1).astype(jnp.float32), precision=HI),
            jnp.dot(tile_pack, (tile_owner % group_size + 1).astype(jnp.float32), precision=HI),
        ],
        axis=1,
    )
    info = jnp.pad(info, ((0, 0), (0, cycle_len - 2))).reshape(peer_count, cap, cycle_len)
    face_width = lev_dev * cycle_len

    pick = face_matrix(side_len, cell_count)
    for step_index in range(STEPS):
        if step_index == 0:
            solved = column_solve(column_mixing, right=right)
            deferred, solved = lax.optimization_barrier((deferred, solved))
            flows = ring_columns(deferred[0], lev_index, lev_groups).reshape(2, levels * own, cell_count)
            column_survive = ring_columns(deferred[1], lev_index, lev_groups)
            ep = ring_columns(deferred[2], lev_index, lev_groups).reshape(levels)
        else:
            solved, grad_step = column_solve(column_mixing, ep=ep, adjoint=adjoint, survive=column_survive)
            mine = lax.dynamic_slice_in_dim(grad_sum, lev_index * own, own)
            grad_sum = lax.dynamic_update_slice_in_dim(grad_sum, mine + grad_step, lev_index * own, 0)
        flat = solved.reshape(levels * own, cell_count)
        cycle_out = jnp.dot(flat, pick, precision=HI).reshape(levels, own, cycle_len) * own_weight[None]
        by_level = lax.all_to_all(cycle_out, "lev", split_axis=0, concat_axis=1, tiled=True)
        sent = jnp.einsum("sb,lbk->slk", face_pack, by_level, precision=HI)
        sent = sent.reshape(peer_count, cap, face_width)
        if step_index == 0:
            sent = jnp.concatenate([sent, info], axis=2)
        if step_index == STEPS - 1:
            tile_sent = jnp.dot(tile_pack, grad_sum, precision=HI).reshape(peer_count, cap, cell_count)
            sent = jnp.concatenate([sent, tile_sent], axis=2)
        got = lax.all_to_all(sent, "blk", split_axis=0, concat_axis=0, tiled=True)
        got = got.reshape(peer_count * cap, -1)
        if step_index == 0:
            face_take = (
                got[:, face_width][None, :]
                == (jnp.arange(blocks, dtype=jnp.int32) + 1).astype(jnp.float32)[:, None]
            ).astype(jnp.float32)
            tile_take = (
                got[:, face_width + 1][None, :]
                == (jnp.arange(group_size, dtype=jnp.int32) + 1).astype(jnp.float32)[:, None]
            ).astype(jnp.float32)
        if step_index == STEPS - 1:
            tile_got = got[:, face_width:]
        got = got[:, :face_width].reshape(peer_count * cap, lev_dev, cycle_len)
        arrivals = jnp.einsum("ts,slk->ltk", face_take, got, precision=HI)
        arrivals = to_columns(arrivals).reshape(levels * own, cycle_len)
        added = jnp.dot(arrivals, pick.T, precision=HI)
        adjoint = advect(side_len, row_steps, flat, flows[0], flows[1], added).reshape(levels, own, cell_count)

    tile_parts = jnp.dot(tile_take, tile_got, precision=HI)
    tile_rows = group_size // lev_groups
    packed = jnp.concatenate(
        [
            adjoint.reshape(lev_groups, lev_dev * own, cell_count),
            tile_parts.reshape(lev_groups, tile_rows, cell_count),
        ],
        axis=1,
    )
    packed = lax.all_to_all(packed, "lev", split_axis=0, concat_axis=0, tiled=True)
    tile_grad = jnp.sum(packed[:, lev_dev * own :], axis=0)
    adjoint_out = packed[:, : lev_dev * own].reshape(lev_groups, lev_dev, own, cell_count)
    adjoint_out = adjoint_out.transpose(0, 2, 1, 3).reshape(blocks, lev_dev, cell_count)
    return (adjoint_out, tile_grad)


def solution(mesh):
    placed = (
        P("blk", "lev", None),
        P(None, "blk", "lev", None),
        P("blk", "lev", None),
        P("blk", "lev", None),
        P("blk"),
        P("blk", None),
        P("blk", None),
        P("blk"),
        P("lev"),
        P("blk"),
    )
    return jax.shard_map(
        local,
        mesh=mesh,
        in_specs=placed,
        out_specs=(P("blk", "lev", None), P(("blk", "lev"), None)),
        check_vma=False,
    )
```

```python
import functools

import jax
import jax.numpy as jnp
from jax import lax
from jax.experimental import pallas as pl
from jax.experimental.pallas import tpu as pltpu
from jax.sharding import PartitionSpec as P

RMAX = 4
STEPS = 2
INTERPRET = False
HI = lax.Precision.HIGHEST


def eliminate(right_of, k_ref, x_ref, r_ref):
    level_count = k_ref.shape[0]
    prev_ratio = None
    prev_scaled = None
    for level in range(level_count):
        right = right_of(level)
        lower_k = k_ref[level - 1] if level > 0 else None
        upper_k = k_ref[level] if level < level_count - 1 else None
        if level == 0:
            pivot_val = 1.0 + upper_k
            scaled = right / pivot_val
        else:
            diag_term = 1.0 + lower_k if upper_k is None else 1.0 + lower_k + upper_k
            pivot_val = diag_term + lower_k * prev_ratio
            scaled = (right + lower_k * prev_scaled) / pivot_val
        x_ref[level] = scaled
        if upper_k is not None:
            prev_ratio = -upper_k / pivot_val
            r_ref[level] = prev_ratio
        prev_scaled = scaled
    solved = prev_scaled
    for level in range(level_count - 2, -1, -1):
        solved = x_ref[level] - r_ref[level] * solved
        x_ref[level] = solved


def first_kernel(b_ref, k_ref, x_ref, r_ref):
    eliminate(lambda level: b_ref[level], k_ref, x_ref, r_ref)


def next_kernel(ep_ref, a_ref, s_ref, k_ref, x_ref, g_ref, r_ref):
    level_count = a_ref.shape[0]
    grad = ep_ref[0] * a_ref[0]
    for level in range(1, level_count):
        grad = grad + ep_ref[level] * a_ref[level]
    g_ref[...] = grad
    eliminate(lambda level: a_ref[level] * s_ref[level], k_ref, x_ref, r_ref)


def column_solve(mixing, right=None, ep=None, adjoint=None, survive=None):
    level_count, blocks, cells = mixing.shape
    chunk = 256
    spec = pl.BlockSpec((level_count, blocks, chunk), lambda c: (0, 0, c))
    scratch = [pltpu.VMEM((level_count, blocks, chunk), jnp.float32)]
    solved_shape = jax.ShapeDtypeStruct(mixing.shape, jnp.float32)
    if right is not None:
        return pl.pallas_call(
            first_kernel,
            grid=(cells // chunk,),
            in_specs=[spec, spec],
            out_specs=spec,
            out_shape=solved_shape,
            scratch_shapes=scratch,
            interpret=INTERPRET,
        )(right, mixing)
    return pl.pallas_call(
        next_kernel,
        grid=(cells // chunk,),
        in_specs=[pl.BlockSpec(memory_space=pltpu.SMEM), spec, spec, spec],
        out_specs=[spec, pl.BlockSpec((blocks, chunk), lambda c: (0, c))],
        out_shape=[solved_shape, jax.ShapeDtypeStruct((blocks, cells), jnp.float32)],
        scratch_shapes=scratch,
        interpret=INTERPRET,
    )(ep, adjoint, survive, mixing)


def stencil_kernel(side_len, st_ref, v_ref, e_ref, n_ref, add_ref, o_ref):
    v = v_ref[...]
    east_c = e_ref[...]
    north_c = n_ref[...]
    cells = v.shape[1]
    lane = lax.broadcasted_iota(jnp.int32, v.shape, 1)
    east_ok = lane % side_len != side_len - 1
    north_ok = lane < cells - side_len
    keep = 1.0 - east_c - north_c
    steps = st_ref[...]
    for substep in range(RMAX):
        east_adj = jnp.where(east_ok, pltpu.roll(v, cells - 1, 1), 0.0)
        north_adj = jnp.where(north_ok, pltpu.roll(v, cells - side_len, 1), 0.0)
        moved = keep * v + east_c * east_adj + north_c * north_adj
        v = jnp.where(substep < steps, moved, v)
    o_ref[...] = v + add_ref[...]


def advect(side_len, steps, adjoint, east_c, north_c, added):
    rows, cells = adjoint.shape
    tile = 64
    spec = pl.BlockSpec((tile, cells), lambda r: (r, 0))
    return pl.pallas_call(
        functools.partial(stencil_kernel, side_len),
        grid=(rows // tile,),
        in_specs=[pl.BlockSpec((tile, 1), lambda r: (r, 0)), spec, spec, spec, spec],
        out_specs=spec,
        out_shape=jax.ShapeDtypeStruct(adjoint.shape, jnp.float32),
        interpret=INTERPRET,
    )(steps, adjoint, east_c, north_c, added)


def face_matrix(side_len, cells):
    pos = jnp.arange(side_len, dtype=jnp.int32)
    where = jnp.concatenate([pos, (side_len - 1) * side_len + pos, pos * side_len, pos * side_len + side_len - 1])
    return (jnp.arange(cells, dtype=jnp.int32)[:, None] == where[None, :]).astype(jnp.float32)


def pack_plan(keys, dest_count, cap):
    count = keys.shape[0]
    order = jnp.arange(count, dtype=jnp.int32)
    earlier = (keys[:, None] == keys[None, :]) & (order[None, :] < order[:, None])
    slot = keys * cap + jnp.sum(earlier.astype(jnp.int32), axis=1)
    rows = jnp.arange(dest_count * cap, dtype=jnp.int32)
    return (rows[:, None] == slot[None, :]).astype(jnp.float32)


def to_columns(x):
    return lax.all_to_all(x, "lev", split_axis=x.ndim - 2, concat_axis=x.ndim - 3, tiled=True)


def ring_columns(x, lev_index, lev_groups):
    lead = x.shape[:-3]
    lev_dev, blocks, cells = x.shape[-3:]
    own = blocks // lev_groups
    parts = x.reshape(lead + (lev_dev, lev_groups, own, cells))
    got = []
    for shift in range(lev_groups):
        piece = lax.dynamic_index_in_dim(parts, (lev_index + shift) % lev_groups, axis=len(lead) + 1, keepdims=False)
        if shift:
            ring = [(src, (src + shift) % lev_groups) for src in range(lev_groups)]
            piece = lax.ppermute(piece, "lev", ring)
        got.append(piece)
    got = jnp.stack(got, axis=len(lead))
    order = (lev_index - jnp.arange(lev_groups, dtype=jnp.int32)) % lev_groups
    got = jnp.take(got, order, axis=len(lead))
    return got.reshape(lead + (lev_groups * lev_dev, own, cells))


def ring_sum(x, lev_index, lev_groups):
    total = lax.dynamic_index_in_dim(x, lev_index, axis=x.ndim - 2, keepdims=False)
    for shift in range(1, lev_groups):
        piece = lax.dynamic_index_in_dim(x, (lev_index + shift) % lev_groups, axis=x.ndim - 2, keepdims=False)
        ring = [(src, (src + shift) % lev_groups) for src in range(lev_groups)]
        total = total + lax.ppermute(piece, "lev", ring)
    return total


def local(
    adjoint_in,
    courant,
    mixing,
    oh_rate,
    substeps,
    nest_weight,
    dest_device,
    dest_slot,
    emission_profile,
    tile_owner,
):
    blocks, lev_dev, cell_count = adjoint_in.shape
    cycle_len = nest_weight.shape[1]
    side_len = cycle_len // 4
    peer_count = lax.axis_size("blk")
    lev_groups = lax.axis_size("lev")
    lev_index = lax.axis_index("lev")
    own = blocks // lev_groups
    levels = lev_dev * lev_groups
    cap = 2

    survive = jnp.exp(-oh_rate)
    state = to_columns(jnp.stack([adjoint_in * survive, mixing]).transpose(0, 2, 1, 3))
    right, column_mixing = state[0], state[1]
    ep = jnp.broadcast_to(emission_profile[:, None, None], (lev_dev, lev_groups, 1))
    deferred = (courant.transpose(0, 2, 1, 3), survive.transpose(1, 0, 2), ep)
    grad_sum = jnp.sum(adjoint_in * emission_profile[None, :, None], axis=1)

    own_steps = lax.dynamic_slice_in_dim(substeps, lev_index * own, own)
    row_steps = jnp.tile(own_steps, levels)[:, None]
    own_weight = lax.dynamic_slice_in_dim(nest_weight, lev_index * own, own)

    face_pack = pack_plan(dest_device[:, 0], peer_count, cap)
    tiles_total = blocks * peer_count // 4
    group_size = tiles_total // peer_count
    tile_pack = pack_plan(tile_owner // group_size, peer_count, cap)
    info = jnp.stack(
        [
            jnp.dot(face_pack, (dest_slot + 1).astype(jnp.float32), precision=HI),
            jnp.dot(tile_pack, (tile_owner % group_size + 1).astype(jnp.float32), precision=HI),
        ],
        axis=1,
    )
    info = jnp.pad(info, ((0, 0), (0, cycle_len - 2))).reshape(peer_count, cap, cycle_len)
    face_width = lev_dev * cycle_len

    pick = face_matrix(side_len, cell_count)
    for step_index in range(STEPS):
        if step_index == 0:
            solved = column_solve(column_mixing, right=right)
            deferred, solved = lax.optimization_barrier((deferred, solved))
            flows = ring_columns(deferred[0], lev_index, lev_groups).reshape(2, levels * own, cell_count)
            column_survive = ring_columns(deferred[1], lev_index, lev_groups)
            ep = ring_columns(deferred[2], lev_index, lev_groups).reshape(levels)
        else:
            solved, grad_step = column_solve(column_mixing, ep=ep, adjoint=adjoint, survive=column_survive)
            mine = lax.dynamic_slice_in_dim(grad_sum, lev_index * own, own)
            grad_sum = lax.dynamic_update_slice_in_dim(grad_sum, mine + grad_step, lev_index * own, 0)
        flat = solved.reshape(levels * own, cell_count)
        cycle_out = jnp.dot(flat, pick, precision=HI).reshape(levels, own, cycle_len) * own_weight[None]
        by_level = lax.all_to_all(cycle_out, "lev", split_axis=0, concat_axis=1, tiled=True)
        sent = jnp.einsum("sb,lbk->slk", face_pack, by_level, precision=HI)
        sent = sent.reshape(peer_count, cap, face_width)
        if step_index == 0:
            sent = jnp.concatenate([sent, info], axis=2)
        if step_index == STEPS - 1:
            quarter = ring_sum(grad_sum.reshape(blocks, lev_groups, cell_count // lev_groups), lev_index, lev_groups)
            tile_sent = jnp.dot(tile_pack, quarter, precision=HI).reshape(peer_count, cap, -1)
            sent = jnp.concatenate([sent, tile_sent], axis=2)
        got = lax.all_to_all(sent, "blk", split_axis=0, concat_axis=0, tiled=True)
        got = got.reshape(peer_count * cap, -1)
        if step_index == 0:
            face_take = (
                got[:, face_width][None, :]
                == (jnp.arange(blocks, dtype=jnp.int32) + 1).astype(jnp.float32)[:, None]
            ).astype(jnp.float32)
            tile_take = (
                got[:, face_width + 1][None, :]
                == (jnp.arange(group_size, dtype=jnp.int32) + 1).astype(jnp.float32)[:, None]
            ).astype(jnp.float32)
        if step_index == STEPS - 1:
            tile_got = got[:, face_width:]
        got = got[:, :face_width].reshape(peer_count * cap, lev_dev, cycle_len)
        arrivals = jnp.einsum("ts,slk->ltk", face_take, got, precision=HI)
        arrivals = to_columns(arrivals).reshape(levels * own, cycle_len)
        added = jnp.dot(arrivals, pick.T, precision=HI)
        adjoint = advect(side_len, row_steps, flat, flows[0], flows[1], added).reshape(levels, own, cell_count)

    tile_parts = jnp.dot(tile_take, tile_got, precision=HI)
    tile_rows = group_size // lev_groups
    packed = jnp.concatenate(
        [
            adjoint.reshape(lev_groups, lev_dev * own, cell_count),
            tile_parts.reshape(lev_groups, 1, cell_count),
        ],
        axis=1,
    )
    packed = lax.all_to_all(packed, "lev", split_axis=0, concat_axis=0, tiled=True)
    tile_grad = packed[:, lev_dev * own].reshape(lev_groups, tile_rows, cell_count // lev_groups)
    tile_grad = tile_grad.transpose(1, 0, 2).reshape(tile_rows, cell_count)
    adjoint_out = packed[:, : lev_dev * own].reshape(lev_groups, lev_dev, own, cell_count)
    adjoint_out = adjoint_out.transpose(0, 2, 1, 3).reshape(blocks, lev_dev, cell_count)
    return (adjoint_out, tile_grad)


def solution(mesh):
    placed = (
        P("blk", "lev", None),
        P(None, "blk", "lev", None),
        P("blk", "lev", None),
        P("blk", "lev", None),
        P("blk"),
        P("blk", None),
        P("blk", None),
        P("blk"),
        P("lev"),
        P("blk"),
    )
    return jax.shard_map(
        local,
        mesh=mesh,
        in_specs=placed,
        out_specs=(P("blk", "lev", None), P(("blk", "lev"), None)),
        check_vma=False,
    )
```

```python
import functools

import jax
import jax.numpy as jnp
from jax import lax
from jax.experimental import pallas as pl
from jax.experimental.pallas import tpu as pltpu
from jax.sharding import PartitionSpec as P

RMAX = 4
STEPS = 2
INTERPRET = False
HI = lax.Precision.HIGHEST


def eliminate(right_of, k_ref, x_ref, r_ref):
    level_count = k_ref.shape[0]
    prev_ratio = None
    prev_scaled = None
    for level in range(level_count):
        right = right_of(level)
        lower_k = k_ref[level - 1] if level > 0 else None
        upper_k = k_ref[level] if level < level_count - 1 else None
        if level == 0:
            pivot_val = 1.0 + upper_k
            scaled = right / pivot_val
        else:
            diag_term = 1.0 + lower_k if upper_k is None else 1.0 + lower_k + upper_k
            pivot_val = diag_term + lower_k * prev_ratio
            scaled = (right + lower_k * prev_scaled) / pivot_val
        x_ref[level] = scaled
        if upper_k is not None:
            prev_ratio = -upper_k / pivot_val
            r_ref[level] = prev_ratio
        prev_scaled = scaled
    solved = prev_scaled
    for level in range(level_count - 2, -1, -1):
        solved = x_ref[level] - r_ref[level] * solved
        x_ref[level] = solved


def first_kernel(b_ref, k_ref, x_ref, r_ref):
    eliminate(lambda level: b_ref[level], k_ref, x_ref, r_ref)


def next_kernel(ep_ref, a_ref, s_ref, k_ref, x_ref, g_ref, r_ref):
    level_count = a_ref.shape[0]
    grad = ep_ref[0] * a_ref[0]
    for level in range(1, level_count):
        grad = grad + ep_ref[level] * a_ref[level]
    g_ref[...] = grad
    eliminate(lambda level: a_ref[level] * s_ref[level], k_ref, x_ref, r_ref)


def column_solve(mixing, right=None, ep=None, adjoint=None, survive=None):
    level_count, blocks, cells = mixing.shape
    chunk = 256
    spec = pl.BlockSpec((level_count, blocks, chunk), lambda c: (0, 0, c))
    scratch = [pltpu.VMEM((level_count, blocks, chunk), jnp.float32)]
    solved_shape = jax.ShapeDtypeStruct(mixing.shape, jnp.float32)
    if right is not None:
        return pl.pallas_call(
            first_kernel,
            grid=(cells // chunk,),
            in_specs=[spec, spec],
            out_specs=spec,
            out_shape=solved_shape,
            scratch_shapes=scratch,
            interpret=INTERPRET,
        )(right, mixing)
    return pl.pallas_call(
        next_kernel,
        grid=(cells // chunk,),
        in_specs=[pl.BlockSpec(memory_space=pltpu.SMEM), spec, spec, spec],
        out_specs=[spec, pl.BlockSpec((blocks, chunk), lambda c: (0, c))],
        out_shape=[solved_shape, jax.ShapeDtypeStruct((blocks, cells), jnp.float32)],
        scratch_shapes=scratch,
        interpret=INTERPRET,
    )(ep, adjoint, survive, mixing)


def stencil_kernel(side_len, st_ref, v_ref, e_ref, n_ref, o_ref):
    v = v_ref[...]
    east_c = e_ref[...]
    north_c = n_ref[...]
    cells = v.shape[1]
    lane = lax.broadcasted_iota(jnp.int32, v.shape, 1)
    east_ok = lane % side_len != side_len - 1
    north_ok = lane < cells - side_len
    keep = 1.0 - east_c - north_c
    steps = st_ref[...]
    for substep in range(RMAX):
        east_adj = jnp.where(east_ok, pltpu.roll(v, cells - 1, 1), 0.0)
        north_adj = jnp.where(north_ok, pltpu.roll(v, cells - side_len, 1), 0.0)
        moved = keep * v + east_c * east_adj + north_c * north_adj
        v = jnp.where(substep < steps, moved, v)
    o_ref[...] = v


def advect(side_len, steps, adjoint, east_c, north_c):
    rows, cells = adjoint.shape
    tile = 64
    spec = pl.BlockSpec((tile, cells), lambda r: (r, 0))
    return pl.pallas_call(
        functools.partial(stencil_kernel, side_len),
        grid=(rows // tile,),
        in_specs=[pl.BlockSpec((tile, 1), lambda r: (r, 0)), spec, spec, spec],
        out_specs=spec,
        out_shape=jax.ShapeDtypeStruct(adjoint.shape, jnp.float32),
        interpret=INTERPRET,
    )(steps, adjoint, east_c, north_c)


def face_matrix(side_len, cells):
    pos = jnp.arange(side_len, dtype=jnp.int32)
    where = jnp.concatenate([pos, (side_len - 1) * side_len + pos, pos * side_len, pos * side_len + side_len - 1])
    return (jnp.arange(cells, dtype=jnp.int32)[:, None] == where[None, :]).astype(jnp.float32)


def pack_plan(keys, dest_count, cap):
    count = keys.shape[0]
    order = jnp.arange(count, dtype=jnp.int32)
    earlier = (keys[:, None] == keys[None, :]) & (order[None, :] < order[:, None])
    slot = keys * cap + jnp.sum(earlier.astype(jnp.int32), axis=1)
    rows = jnp.arange(dest_count * cap, dtype=jnp.int32)
    return (rows[:, None] == slot[None, :]).astype(jnp.float32)


def to_columns(x):
    return lax.all_to_all(x, "lev", split_axis=x.ndim - 2, concat_axis=x.ndim - 3, tiled=True)


def ring_columns(x, lev_index, lev_groups):
    lead = x.shape[:-3]
    lev_dev, blocks, cells = x.shape[-3:]
    own = blocks // lev_groups
    parts = x.reshape(lead + (lev_dev, lev_groups, own, cells))
    got = []
    for shift in range(lev_groups):
        piece = lax.dynamic_index_in_dim(parts, (lev_index + shift) % lev_groups, axis=len(lead) + 1, keepdims=False)
        if shift:
            ring = [(src, (src + shift) % lev_groups) for src in range(lev_groups)]
            piece = lax.ppermute(piece, "lev", ring)
        got.append(piece)
    got = jnp.stack(got, axis=len(lead))
    order = (lev_index - jnp.arange(lev_groups, dtype=jnp.int32)) % lev_groups
    got = jnp.take(got, order, axis=len(lead))
    return got.reshape(lead + (lev_groups * lev_dev, own, cells))


def ring_exchange(x, lev_index, lev_groups):
    got = []
    for shift in range(lev_groups):
        piece = lax.dynamic_index_in_dim(x, (lev_index + shift) % lev_groups, axis=0, keepdims=False)
        if shift:
            ring = [(src, (src + shift) % lev_groups) for src in range(lev_groups)]
            piece = lax.ppermute(piece, "lev", ring)
        got.append(piece)
    got = jnp.stack(got, axis=0)
    order = (lev_index - jnp.arange(lev_groups, dtype=jnp.int32)) % lev_groups
    return jnp.take(got, order, axis=0)


def ring_sum(x, lev_index, lev_groups):
    total = lax.dynamic_index_in_dim(x, lev_index, axis=x.ndim - 2, keepdims=False)
    for shift in range(1, lev_groups):
        piece = lax.dynamic_index_in_dim(x, (lev_index + shift) % lev_groups, axis=x.ndim - 2, keepdims=False)
        ring = [(src, (src + shift) % lev_groups) for src in range(lev_groups)]
        total = total + lax.ppermute(piece, "lev", ring)
    return total


def local(
    adjoint_in,
    courant,
    mixing,
    oh_rate,
    substeps,
    nest_weight,
    dest_device,
    dest_slot,
    emission_profile,
    tile_owner,
):
    blocks, lev_dev, cell_count = adjoint_in.shape
    cycle_len = nest_weight.shape[1]
    side_len = cycle_len // 4
    peer_count = lax.axis_size("blk")
    lev_groups = lax.axis_size("lev")
    lev_index = lax.axis_index("lev")
    own = blocks // lev_groups
    levels = lev_dev * lev_groups
    cap = 2

    survive = jnp.exp(-oh_rate)
    state = to_columns(jnp.stack([adjoint_in * survive, mixing]).transpose(0, 2, 1, 3))
    right, column_mixing = state[0], state[1]
    ep = jnp.broadcast_to(emission_profile[:, None, None], (lev_dev, lev_groups, 1))
    deferred = (courant.transpose(0, 2, 1, 3), survive.transpose(1, 0, 2), ep)
    grad_sum = jnp.sum(adjoint_in * emission_profile[None, :, None], axis=1)

    own_steps = lax.dynamic_slice_in_dim(substeps, lev_index * own, own)
    row_steps = jnp.tile(own_steps, levels)[:, None]
    own_weight = lax.dynamic_slice_in_dim(nest_weight, lev_index * own, own)

    face_pack = pack_plan(dest_device[:, 0], peer_count, cap)
    tiles_total = blocks * peer_count // 4
    group_size = tiles_total // peer_count
    tile_pack = pack_plan(tile_owner // group_size, peer_count, cap)
    info = jnp.stack(
        [
            jnp.dot(face_pack, (dest_slot + 1).astype(jnp.float32), precision=HI),
            jnp.dot(tile_pack, (tile_owner % group_size + 1).astype(jnp.float32), precision=HI),
        ],
        axis=1,
    )
    info = jnp.pad(info, ((0, 0), (0, cycle_len - 2))).reshape(peer_count, cap, cycle_len)
    face_width = lev_dev * cycle_len

    pick = face_matrix(side_len, cell_count)
    for step_index in range(STEPS):
        if step_index == 0:
            solved = column_solve(column_mixing, right=right)
            deferred, solved = lax.optimization_barrier((deferred, solved))
            flows = ring_columns(deferred[0], lev_index, lev_groups).reshape(2, levels * own, cell_count)
            column_survive = ring_columns(deferred[1], lev_index, lev_groups)
            ep = ring_columns(deferred[2], lev_index, lev_groups).reshape(levels)
        else:
            solved, grad_step = column_solve(column_mixing, ep=ep, adjoint=adjoint, survive=column_survive)
            mine = lax.dynamic_slice_in_dim(grad_sum, lev_index * own, own)
            grad_sum = lax.dynamic_update_slice_in_dim(grad_sum, mine + grad_step, lev_index * own, 0)
        flat = solved.reshape(levels * own, cell_count)
        cycle_out = jnp.dot(flat, pick, precision=HI).reshape(levels, own, cycle_len) * own_weight[None]
        by_level = lax.all_to_all(cycle_out, "lev", split_axis=0, concat_axis=1, tiled=True)
        sent = jnp.einsum("sb,lbk->slk", face_pack, by_level, precision=HI)
        sent = sent.reshape(peer_count, cap, face_width)
        if step_index == 0:
            sent = jnp.concatenate([sent, info], axis=2)
        if step_index == STEPS - 1:
            quarter = ring_sum(grad_sum.reshape(blocks, lev_groups, cell_count // lev_groups), lev_index, lev_groups)
            tile_sent = jnp.dot(tile_pack, quarter, precision=HI).reshape(peer_count, cap, -1)
            sent = jnp.concatenate([sent, tile_sent], axis=2)
        got = lax.all_to_all(sent, "blk", split_axis=0, concat_axis=0, tiled=True)
        got = got.reshape(peer_count * cap, -1)
        if step_index == 0:
            face_take = (
                got[:, face_width][None, :]
                == (jnp.arange(blocks, dtype=jnp.int32) + 1).astype(jnp.float32)[:, None]
            ).astype(jnp.float32)
            tile_take = (
                got[:, face_width + 1][None, :]
                == (jnp.arange(group_size, dtype=jnp.int32) + 1).astype(jnp.float32)[:, None]
            ).astype(jnp.float32)
        if step_index == STEPS - 1:
            tile_got = got[:, face_width:]
        got = got[:, :face_width].reshape(peer_count * cap, lev_dev, cycle_len)
        arrivals = jnp.einsum("ts,slk->ltk", face_take, got, precision=HI)
        advected = advect(side_len, row_steps, flat, flows[0], flows[1])
        if step_index < STEPS - 1:
            arrivals = to_columns(arrivals).reshape(levels * own, cycle_len)
            added = jnp.dot(arrivals, pick.T, precision=HI)
            adjoint = (advected + added).reshape(levels, own, cell_count)

    by_dest = advected.reshape(lev_groups, lev_dev, own, cell_count)
    by_src = ring_exchange(by_dest, lev_index, lev_groups)
    advected = by_src.transpose(1, 0, 2, 3).reshape(lev_dev, blocks, cell_count)
    added = jnp.dot(arrivals.reshape(lev_dev * blocks, cycle_len), pick.T, precision=HI)
    adjoint_out = (advected + added.reshape(lev_dev, blocks, cell_count)).transpose(1, 0, 2)

    tile_parts = jnp.dot(tile_take, tile_got, precision=HI)
    tile_rows = group_size // lev_groups
    tile_parts = tile_parts.reshape(lev_groups, tile_rows, cell_count // lev_groups)
    tile_grad = ring_exchange(tile_parts, lev_index, lev_groups)
    tile_grad = tile_grad.transpose(1, 0, 2).reshape(tile_rows, cell_count)
    return (adjoint_out, tile_grad)


def solution(mesh):
    placed = (
        P("blk", "lev", None),
        P(None, "blk", "lev", None),
        P("blk", "lev", None),
        P("blk", "lev", None),
        P("blk"),
        P("blk", None),
        P("blk", None),
        P("blk"),
        P("lev"),
        P("blk"),
    )
    return jax.shard_map(
        local,
        mesh=mesh,
        in_specs=placed,
        out_specs=(P("blk", "lev", None), P(("blk", "lev"), None)),
        check_vma=False,
    )
```

```python
import functools

import jax
import jax.numpy as jnp
from jax import lax
from jax.experimental import pallas as pl
from jax.experimental.pallas import tpu as pltpu
from jax.sharding import PartitionSpec as P

RMAX = 4
STEPS = 2
INTERPRET = False
HI = lax.Precision.HIGHEST


def eliminate(right_of, k_ref, x_ref, r_ref):
    level_count = k_ref.shape[0]
    prev_ratio = None
    prev_scaled = None
    for level in range(level_count):
        right = right_of(level)
        lower_k = k_ref[level - 1] if level > 0 else None
        upper_k = k_ref[level] if level < level_count - 1 else None
        if level == 0:
            pivot_val = 1.0 + upper_k
            scaled = right / pivot_val
        else:
            diag_term = 1.0 + lower_k if upper_k is None else 1.0 + lower_k + upper_k
            pivot_val = diag_term + lower_k * prev_ratio
            scaled = (right + lower_k * prev_scaled) / pivot_val
        x_ref[level] = scaled
        if upper_k is not None:
            prev_ratio = -upper_k / pivot_val
            r_ref[level] = prev_ratio
        prev_scaled = scaled
    solved = prev_scaled
    for level in range(level_count - 2, -1, -1):
        solved = x_ref[level] - r_ref[level] * solved
        x_ref[level] = solved


def first_kernel(b_ref, k_ref, x_ref, r_ref):
    eliminate(lambda level: b_ref[level], k_ref, x_ref, r_ref)


def next_kernel(ep_ref, a_ref, s_ref, k_ref, x_ref, g_ref, r_ref):
    level_count = a_ref.shape[0]
    grad = ep_ref[0] * a_ref[0]
    for level in range(1, level_count):
        grad = grad + ep_ref[level] * a_ref[level]
    g_ref[...] = grad
    eliminate(lambda level: a_ref[level] * s_ref[level], k_ref, x_ref, r_ref)


def column_solve(mixing, right=None, ep=None, adjoint=None, survive=None):
    level_count, blocks, cells = mixing.shape
    chunk = 256
    spec = pl.BlockSpec((level_count, blocks, chunk), lambda c: (0, 0, c))
    scratch = [pltpu.VMEM((level_count, blocks, chunk), jnp.float32)]
    solved_shape = jax.ShapeDtypeStruct(mixing.shape, jnp.float32)
    if right is not None:
        return pl.pallas_call(
            first_kernel,
            grid=(cells // chunk,),
            in_specs=[spec, spec],
            out_specs=spec,
            out_shape=solved_shape,
            scratch_shapes=scratch,
            interpret=INTERPRET,
        )(right, mixing)
    return pl.pallas_call(
        next_kernel,
        grid=(cells // chunk,),
        in_specs=[pl.BlockSpec(memory_space=pltpu.SMEM), spec, spec, spec],
        out_specs=[spec, pl.BlockSpec((blocks, chunk), lambda c: (0, c))],
        out_shape=[solved_shape, jax.ShapeDtypeStruct((blocks, cells), jnp.float32)],
        scratch_shapes=scratch,
        interpret=INTERPRET,
    )(ep, adjoint, survive, mixing)


def stencil_kernel(side_len, st_ref, v_ref, e_ref, n_ref, o_ref):
    v = v_ref[...]
    east_c = e_ref[...]
    north_c = n_ref[...]
    cells = v.shape[1]
    lane = lax.broadcasted_iota(jnp.int32, v.shape, 1)
    east_ok = lane % side_len != side_len - 1
    north_ok = lane < cells - side_len
    keep = 1.0 - east_c - north_c
    steps = st_ref[...]
    for substep in range(RMAX):
        east_adj = jnp.where(east_ok, pltpu.roll(v, cells - 1, 1), 0.0)
        north_adj = jnp.where(north_ok, pltpu.roll(v, cells - side_len, 1), 0.0)
        moved = keep * v + east_c * east_adj + north_c * north_adj
        v = jnp.where(substep < steps, moved, v)
    o_ref[...] = v


def advect(side_len, steps, adjoint, east_c, north_c):
    rows, cells = adjoint.shape
    tile = 64
    spec = pl.BlockSpec((tile, cells), lambda r: (r, 0))
    return pl.pallas_call(
        functools.partial(stencil_kernel, side_len),
        grid=(rows // tile,),
        in_specs=[pl.BlockSpec((tile, 1), lambda r: (r, 0)), spec, spec, spec],
        out_specs=spec,
        out_shape=jax.ShapeDtypeStruct(adjoint.shape, jnp.float32),
        interpret=INTERPRET,
    )(steps, adjoint, east_c, north_c)


def face_matrix(side_len, cells):
    pos = jnp.arange(side_len, dtype=jnp.int32)
    where = jnp.concatenate([pos, (side_len - 1) * side_len + pos, pos * side_len, pos * side_len + side_len - 1])
    return (jnp.arange(cells, dtype=jnp.int32)[:, None] == where[None, :]).astype(jnp.float32)


def pack_plan(keys, dest_count, cap):
    count = keys.shape[0]
    order = jnp.arange(count, dtype=jnp.int32)
    earlier = (keys[:, None] == keys[None, :]) & (order[None, :] < order[:, None])
    slot = keys * cap + jnp.sum(earlier.astype(jnp.int32), axis=1)
    rows = jnp.arange(dest_count * cap, dtype=jnp.int32)
    return (rows[:, None] == slot[None, :]).astype(jnp.float32)


def to_columns(x):
    return lax.all_to_all(x, "lev", split_axis=x.ndim - 2, concat_axis=x.ndim - 3, tiled=True)


def ring_columns(x, lev_index, lev_groups):
    lead = x.shape[:-3]
    lev_dev, blocks, cells = x.shape[-3:]
    own = blocks // lev_groups
    parts = x.reshape(lead + (lev_dev, lev_groups, own, cells))
    got = []
    for shift in range(lev_groups):
        piece = lax.dynamic_index_in_dim(parts, (lev_index + shift) % lev_groups, axis=len(lead) + 1, keepdims=False)
        if shift:
            ring = [(src, (src + shift) % lev_groups) for src in range(lev_groups)]
            piece = lax.ppermute(piece, "lev", ring)
        got.append(piece)
    got = jnp.stack(got, axis=len(lead))
    order = (lev_index - jnp.arange(lev_groups, dtype=jnp.int32)) % lev_groups
    got = jnp.take(got, order, axis=len(lead))
    return got.reshape(lead + (lev_groups * lev_dev, own, cells))


def ring_exchange(x, lev_index, lev_groups):
    got = []
    for shift in range(lev_groups):
        piece = lax.dynamic_index_in_dim(x, (lev_index + shift) % lev_groups, axis=0, keepdims=False)
        if shift:
            ring = [(src, (src + shift) % lev_groups) for src in range(lev_groups)]
            piece = lax.ppermute(piece, "lev", ring)
        got.append(piece)
    got = jnp.stack(got, axis=0)
    order = (lev_index - jnp.arange(lev_groups, dtype=jnp.int32)) % lev_groups
    return jnp.take(got, order, axis=0)


def ring_sum(x, lev_index, lev_groups):
    total = lax.dynamic_index_in_dim(x, lev_index, axis=x.ndim - 2, keepdims=False)
    for shift in range(1, lev_groups):
        piece = lax.dynamic_index_in_dim(x, (lev_index + shift) % lev_groups, axis=x.ndim - 2, keepdims=False)
        ring = [(src, (src + shift) % lev_groups) for src in range(lev_groups)]
        total = total + lax.ppermute(piece, "lev", ring)
    return total


def local(
    adjoint_in,
    courant,
    mixing,
    oh_rate,
    substeps,
    nest_weight,
    dest_device,
    dest_slot,
    emission_profile,
    tile_owner,
):
    blocks, lev_dev, cell_count = adjoint_in.shape
    cycle_len = nest_weight.shape[1]
    side_len = cycle_len // 4
    peer_count = lax.axis_size("blk")
    lev_groups = lax.axis_size("lev")
    lev_index = lax.axis_index("lev")
    own = blocks // lev_groups
    levels = lev_dev * lev_groups
    cap = 2

    survive = jnp.exp(-oh_rate)
    state = to_columns(jnp.stack([adjoint_in * survive, mixing]).transpose(0, 2, 1, 3))
    right, column_mixing = state[0], state[1]
    ep = jnp.broadcast_to(emission_profile[:, None, None], (lev_dev, lev_groups, 1))
    ep = ring_columns(ep, lev_index, lev_groups).reshape(levels)
    deferred = (courant.transpose(0, 2, 1, 3), survive.transpose(1, 0, 2))
    grad_sum = jnp.sum(adjoint_in * emission_profile[None, :, None], axis=1)

    own_steps = lax.dynamic_slice_in_dim(substeps, lev_index * own, own)
    row_steps = jnp.tile(own_steps, levels)[:, None]
    own_weight = lax.dynamic_slice_in_dim(nest_weight, lev_index * own, own)

    face_pack = pack_plan(dest_device[:, 0], peer_count, cap)
    tiles_total = blocks * peer_count // 4
    group_size = tiles_total // peer_count
    tile_pack = pack_plan(tile_owner // group_size, peer_count, cap)
    info = jnp.stack(
        [
            jnp.dot(face_pack, (dest_slot + 1).astype(jnp.float32), precision=HI),
            jnp.dot(tile_pack, (tile_owner % group_size + 1).astype(jnp.float32), precision=HI),
        ],
        axis=1,
    )
    info = jnp.pad(info, ((0, 0), (0, cycle_len - 2))).reshape(peer_count, cap, cycle_len)
    face_width = lev_dev * cycle_len

    pick = face_matrix(side_len, cell_count)
    for step_index in range(STEPS):
        if step_index == 0:
            solved = column_solve(column_mixing, right=right)
            deferred, solved = lax.optimization_barrier((deferred, solved))
            flows = ring_columns(deferred[0], lev_index, lev_groups).reshape(2, levels * own, cell_count)
            column_survive = ring_columns(deferred[1], lev_index, lev_groups)
        else:
            solved, grad_step = column_solve(column_mixing, ep=ep, adjoint=adjoint, survive=column_survive)
            mine = lax.dynamic_slice_in_dim(grad_sum, lev_index * own, own)
            grad_sum = lax.dynamic_update_slice_in_dim(grad_sum, mine + grad_step, lev_index * own, 0)
        flat = solved.reshape(levels * own, cell_count)
        cycle_out = jnp.dot(flat, pick, precision=HI).reshape(levels, own, cycle_len) * own_weight[None]
        by_level = lax.all_to_all(cycle_out, "lev", split_axis=0, concat_axis=1, tiled=True)
        sent = jnp.einsum("sb,lbk->slk", face_pack, by_level, precision=HI)
        sent = sent.reshape(peer_count, cap, face_width)
        if step_index == 0:
            sent = jnp.concatenate([sent, info], axis=2)
        if step_index == STEPS - 1:
            quarter = ring_sum(grad_sum.reshape(blocks, lev_groups, cell_count // lev_groups), lev_index, lev_groups)
            tile_sent = jnp.dot(tile_pack, quarter, precision=HI).reshape(peer_count, cap, -1)
            sent = jnp.concatenate([sent, tile_sent], axis=2)
        got = lax.all_to_all(sent, "blk", split_axis=0, concat_axis=0, tiled=True)
        got = got.reshape(peer_count * cap, -1)
        if step_index == 0:
            face_take = (
                got[:, face_width][None, :]
                == (jnp.arange(blocks, dtype=jnp.int32) + 1).astype(jnp.float32)[:, None]
            ).astype(jnp.float32)
            tile_take = (
                got[:, face_width + 1][None, :]
                == (jnp.arange(group_size, dtype=jnp.int32) + 1).astype(jnp.float32)[:, None]
            ).astype(jnp.float32)
        if step_index == STEPS - 1:
            tile_got = got[:, face_width:]
        got = got[:, :face_width].reshape(peer_count * cap, lev_dev, cycle_len)
        arrivals = jnp.einsum("ts,slk->ltk", face_take, got, precision=HI)
        advected = advect(side_len, row_steps, flat, flows[0], flows[1])
        if step_index < STEPS - 1:
            arrivals = to_columns(arrivals).reshape(levels * own, cycle_len)
            added = jnp.dot(arrivals, pick.T, precision=HI)
            adjoint = (advected + added).reshape(levels, own, cell_count)

    by_dest = advected.reshape(lev_groups, lev_dev, own, cell_count)
    by_src = ring_exchange(by_dest, lev_index, lev_groups)
    advected = by_src.transpose(1, 0, 2, 3).reshape(lev_dev, blocks, cell_count)
    added = jnp.dot(arrivals.reshape(lev_dev * blocks, cycle_len), pick.T, precision=HI)
    adjoint_out = (advected + added.reshape(lev_dev, blocks, cell_count)).transpose(1, 0, 2)

    tile_parts = jnp.dot(tile_take, tile_got, precision=HI)
    tile_rows = group_size // lev_groups
    tile_parts = tile_parts.reshape(lev_groups, tile_rows, cell_count // lev_groups)
    tile_grad = ring_exchange(tile_parts, lev_index, lev_groups)
    tile_grad = tile_grad.transpose(1, 0, 2).reshape(tile_rows, cell_count)
    return (adjoint_out, tile_grad)


def solution(mesh):
    placed = (
        P("blk", "lev", None),
        P(None, "blk", "lev", None),
        P("blk", "lev", None),
        P("blk", "lev", None),
        P("blk"),
        P("blk", None),
        P("blk", None),
        P("blk"),
        P("lev"),
        P("blk"),
    )
    return jax.shard_map(
        local,
        mesh=mesh,
        in_specs=placed,
        out_specs=(P("blk", "lev", None), P(("blk", "lev"), None)),
        check_vma=False,
    )
```

```python
import functools

import jax
import jax.numpy as jnp
from jax import lax
from jax.experimental import pallas as pl
from jax.experimental.pallas import tpu as pltpu
from jax.sharding import PartitionSpec as P

RMAX = 4
STEPS = 2
INTERPRET = False
HI = lax.Precision.HIGHEST


def eliminate(right_of, k_ref, x_ref, r_ref):
    level_count = k_ref.shape[0]
    prev_ratio = None
    prev_scaled = None
    for level in range(level_count):
        right = right_of(level)
        lower_k = k_ref[level - 1] if level > 0 else None
        upper_k = k_ref[level] if level < level_count - 1 else None
        if level == 0:
            pivot_val = 1.0 + upper_k
            scaled = right / pivot_val
        else:
            diag_term = 1.0 + lower_k if upper_k is None else 1.0 + lower_k + upper_k
            pivot_val = diag_term + lower_k * prev_ratio
            scaled = (right + lower_k * prev_scaled) / pivot_val
        x_ref[level] = scaled
        if upper_k is not None:
            prev_ratio = -upper_k / pivot_val
            r_ref[level] = prev_ratio
        prev_scaled = scaled
    solved = prev_scaled
    for level in range(level_count - 2, -1, -1):
        solved = x_ref[level] - r_ref[level] * solved
        x_ref[level] = solved


def first_kernel(b_ref, k_ref, x_ref, r_ref):
    eliminate(lambda level: b_ref[level], k_ref, x_ref, r_ref)


def next_kernel(ep_ref, a_ref, s_ref, k_ref, x_ref, g_ref, r_ref):
    level_count = a_ref.shape[0]
    grad = ep_ref[0] * a_ref[0]
    for level in range(1, level_count):
        grad = grad + ep_ref[level] * a_ref[level]
    g_ref[...] = grad
    eliminate(lambda level: a_ref[level] * s_ref[level], k_ref, x_ref, r_ref)


def column_solve(mixing, right=None, ep=None, adjoint=None, survive=None):
    level_count, blocks, cells = mixing.shape
    chunk = 256
    spec = pl.BlockSpec((level_count, blocks, chunk), lambda c: (0, 0, c))
    scratch = [pltpu.VMEM((level_count, blocks, chunk), jnp.float32)]
    solved_shape = jax.ShapeDtypeStruct(mixing.shape, jnp.float32)
    if right is not None:
        return pl.pallas_call(
            first_kernel,
            grid=(cells // chunk,),
            in_specs=[spec, spec],
            out_specs=spec,
            out_shape=solved_shape,
            scratch_shapes=scratch,
            interpret=INTERPRET,
        )(right, mixing)
    return pl.pallas_call(
        next_kernel,
        grid=(cells // chunk,),
        in_specs=[pl.BlockSpec(memory_space=pltpu.SMEM), spec, spec, spec],
        out_specs=[spec, pl.BlockSpec((blocks, chunk), lambda c: (0, c))],
        out_shape=[solved_shape, jax.ShapeDtypeStruct((blocks, cells), jnp.float32)],
        scratch_shapes=scratch,
        interpret=INTERPRET,
    )(ep, adjoint, survive, mixing)


def stencil_kernel(side_len, st_ref, v_ref, e_ref, n_ref, o_ref):
    v = v_ref[...]
    east_c = e_ref[...]
    north_c = n_ref[...]
    cells = v.shape[1]
    lane = lax.broadcasted_iota(jnp.int32, v.shape, 1)
    east_ok = lane % side_len != side_len - 1
    north_ok = lane < cells - side_len
    keep = 1.0 - east_c - north_c
    steps = st_ref[...]
    for substep in range(RMAX):
        east_adj = jnp.where(east_ok, pltpu.roll(v, cells - 1, 1), 0.0)
        north_adj = jnp.where(north_ok, pltpu.roll(v, cells - side_len, 1), 0.0)
        moved = keep * v + east_c * east_adj + north_c * north_adj
        v = jnp.where(substep < steps, moved, v)
    o_ref[...] = v


def advect(side_len, steps, adjoint, east_c, north_c):
    rows, cells = adjoint.shape
    tile = 64
    spec = pl.BlockSpec((tile, cells), lambda r: (r, 0))
    return pl.pallas_call(
        functools.partial(stencil_kernel, side_len),
        grid=(rows // tile,),
        in_specs=[pl.BlockSpec((tile, 1), lambda r: (r, 0)), spec, spec, spec],
        out_specs=spec,
        out_shape=jax.ShapeDtypeStruct(adjoint.shape, jnp.float32),
        interpret=INTERPRET,
    )(steps, adjoint, east_c, north_c)


def face_matrix(side_len, cells):
    pos = jnp.arange(side_len, dtype=jnp.int32)
    where = jnp.concatenate([pos, (side_len - 1) * side_len + pos, pos * side_len, pos * side_len + side_len - 1])
    return (jnp.arange(cells, dtype=jnp.int32)[:, None] == where[None, :]).astype(jnp.float32)


def pack_plan(keys, dest_count, cap):
    count = keys.shape[0]
    order = jnp.arange(count, dtype=jnp.int32)
    earlier = (keys[:, None] == keys[None, :]) & (order[None, :] < order[:, None])
    slot = keys * cap + jnp.sum(earlier.astype(jnp.int32), axis=1)
    rows = jnp.arange(dest_count * cap, dtype=jnp.int32)
    return (rows[:, None] == slot[None, :]).astype(jnp.float32)


def to_columns(x):
    return lax.all_to_all(x, "lev", split_axis=x.ndim - 2, concat_axis=x.ndim - 3, tiled=True)


def ring_columns(x, lev_index, lev_groups):
    lead = x.shape[:-3]
    lev_dev, blocks, cells = x.shape[-3:]
    own = blocks // lev_groups
    parts = x.reshape(lead + (lev_dev, lev_groups, own, cells))
    got = []
    for shift in range(lev_groups):
        piece = lax.dynamic_index_in_dim(parts, (lev_index + shift) % lev_groups, axis=len(lead) + 1, keepdims=False)
        if shift:
            ring = [(src, (src + shift) % lev_groups) for src in range(lev_groups)]
            piece = lax.ppermute(piece, "lev", ring)
        got.append(piece)
    got = jnp.stack(got, axis=len(lead))
    order = (lev_index - jnp.arange(lev_groups, dtype=jnp.int32)) % lev_groups
    got = jnp.take(got, order, axis=len(lead))
    return got.reshape(lead + (lev_groups * lev_dev, own, cells))


def ring_exchange(x, lev_index, lev_groups):
    got = []
    for shift in range(lev_groups):
        piece = lax.dynamic_index_in_dim(x, (lev_index + shift) % lev_groups, axis=0, keepdims=False)
        if shift:
            ring = [(src, (src + shift) % lev_groups) for src in range(lev_groups)]
            piece = lax.ppermute(piece, "lev", ring)
        got.append(piece)
    got = jnp.stack(got, axis=0)
    order = (lev_index - jnp.arange(lev_groups, dtype=jnp.int32)) % lev_groups
    return jnp.take(got, order, axis=0)


def ring_sum(x, lev_index, lev_groups):
    total = lax.dynamic_index_in_dim(x, lev_index, axis=x.ndim - 2, keepdims=False)
    for shift in range(1, lev_groups):
        piece = lax.dynamic_index_in_dim(x, (lev_index + shift) % lev_groups, axis=x.ndim - 2, keepdims=False)
        ring = [(src, (src + shift) % lev_groups) for src in range(lev_groups)]
        total = total + lax.ppermute(piece, "lev", ring)
    return total


def local(
    adjoint_in,
    courant,
    mixing,
    oh_rate,
    substeps,
    nest_weight,
    dest_device,
    dest_slot,
    emission_profile,
    tile_owner,
):
    blocks, lev_dev, cell_count = adjoint_in.shape
    cycle_len = nest_weight.shape[1]
    side_len = cycle_len // 4
    peer_count = lax.axis_size("blk")
    lev_groups = lax.axis_size("lev")
    lev_index = lax.axis_index("lev")
    own = blocks // lev_groups
    levels = lev_dev * lev_groups
    cap = 2

    survive = jnp.exp(-oh_rate)
    state = to_columns(jnp.stack([adjoint_in * survive, mixing]).transpose(0, 2, 1, 3))
    right, column_mixing = state[0], state[1]
    ep = jnp.broadcast_to(emission_profile[:, None, None], (lev_dev, lev_groups, 1))
    ep = ring_columns(ep, lev_index, lev_groups).reshape(levels)
    deferred = (courant.transpose(0, 2, 1, 3), survive.transpose(1, 0, 2))
    grad_sum = jnp.sum(adjoint_in * emission_profile[None, :, None], axis=1)

    own_steps = lax.dynamic_slice_in_dim(substeps, lev_index * own, own)
    row_steps = jnp.tile(own_steps, levels)[:, None]
    own_weight = lax.dynamic_slice_in_dim(nest_weight, lev_index * own, own)

    face_pack = pack_plan(dest_device[:, 0], peer_count, cap)
    tiles_total = blocks * peer_count // 4
    group_size = tiles_total // peer_count
    tile_pack = pack_plan(tile_owner // group_size, peer_count, cap)
    info = jnp.stack(
        [
            jnp.dot(face_pack, (dest_slot + 1).astype(jnp.float32), precision=HI),
            jnp.dot(tile_pack, (tile_owner % group_size + 1).astype(jnp.float32), precision=HI),
        ],
        axis=1,
    )
    info = jnp.pad(info, ((0, 0), (0, cycle_len - 2))).reshape(peer_count, cap, cycle_len)
    face_width = lev_dev * cycle_len

    pick = face_matrix(side_len, cell_count)
    for step_index in range(STEPS):
        if step_index == 0:
            solved = column_solve(column_mixing, right=right)
            flows, solved = lax.optimization_barrier((deferred[0], solved))
            flows = ring_columns(flows, lev_index, lev_groups).reshape(2, levels * own, cell_count)
        else:
            solved, grad_step = column_solve(column_mixing, ep=ep, adjoint=adjoint, survive=column_survive)
            mine = lax.dynamic_slice_in_dim(grad_sum, lev_index * own, own)
            grad_sum = lax.dynamic_update_slice_in_dim(grad_sum, mine + grad_step, lev_index * own, 0)
        flat = solved.reshape(levels * own, cell_count)
        cycle_out = jnp.dot(flat, pick, precision=HI).reshape(levels, own, cycle_len) * own_weight[None]
        by_level = lax.all_to_all(cycle_out, "lev", split_axis=0, concat_axis=1, tiled=True)
        if step_index == 0:
            column_survive, by_level = lax.optimization_barrier((deferred[1], by_level))
            column_survive = ring_columns(column_survive, lev_index, lev_groups)
        sent = jnp.einsum("sb,lbk->slk", face_pack, by_level, precision=HI)
        sent = sent.reshape(peer_count, cap, face_width)
        if step_index == 0:
            sent = jnp.concatenate([sent, info], axis=2)
        if step_index == STEPS - 1:
            quarter = ring_sum(grad_sum.reshape(blocks, lev_groups, cell_count // lev_groups), lev_index, lev_groups)
            tile_sent = jnp.dot(tile_pack, quarter, precision=HI).reshape(peer_count, cap, -1)
            sent = jnp.concatenate([sent, tile_sent], axis=2)
        got = lax.all_to_all(sent, "blk", split_axis=0, concat_axis=0, tiled=True)
        got = got.reshape(peer_count * cap, -1)
        if step_index == 0:
            face_take = (
                got[:, face_width][None, :]
                == (jnp.arange(blocks, dtype=jnp.int32) + 1).astype(jnp.float32)[:, None]
            ).astype(jnp.float32)
            tile_take = (
                got[:, face_width + 1][None, :]
                == (jnp.arange(group_size, dtype=jnp.int32) + 1).astype(jnp.float32)[:, None]
            ).astype(jnp.float32)
        if step_index == STEPS - 1:
            tile_got = got[:, face_width:]
        got = got[:, :face_width].reshape(peer_count * cap, lev_dev, cycle_len)
        arrivals = jnp.einsum("ts,slk->ltk", face_take, got, precision=HI)
        advected = advect(side_len, row_steps, flat, flows[0], flows[1])
        if step_index < STEPS - 1:
            arrivals = to_columns(arrivals).reshape(levels * own, cycle_len)
            added = jnp.dot(arrivals, pick.T, precision=HI)
            adjoint = (advected + added).reshape(levels, own, cell_count)

    tile_parts = jnp.dot(tile_take, tile_got, precision=HI)
    tile_rows = group_size // lev_groups
    by_dest = jnp.concatenate(
        [
            advected.reshape(lev_groups, lev_dev * own, cell_count),
            tile_parts.reshape(lev_groups, 1, cell_count),
        ],
        axis=1,
    )
    by_src = ring_exchange(by_dest, lev_index, lev_groups)
    advected = by_src[:, : lev_dev * own].reshape(lev_groups, lev_dev, own, cell_count)
    advected = advected.transpose(1, 0, 2, 3).reshape(lev_dev, blocks, cell_count)
    added = jnp.dot(arrivals.reshape(lev_dev * blocks, cycle_len), pick.T, precision=HI)
    adjoint_out = (advected + added.reshape(lev_dev, blocks, cell_count)).transpose(1, 0, 2)
    tile_grad = by_src[:, lev_dev * own].reshape(lev_groups, tile_rows, cell_count // lev_groups)
    tile_grad = tile_grad.transpose(1, 0, 2).reshape(tile_rows, cell_count)
    return (adjoint_out, tile_grad)


def solution(mesh):
    placed = (
        P("blk", "lev", None),
        P(None, "blk", "lev", None),
        P("blk", "lev", None),
        P("blk", "lev", None),
        P("blk"),
        P("blk", None),
        P("blk", None),
        P("blk"),
        P("lev"),
        P("blk"),
    )
    return jax.shard_map(
        local,
        mesh=mesh,
        in_specs=placed,
        out_specs=(P("blk", "lev", None), P(("blk", "lev"), None)),
        check_vma=False,
    )
```

```python
import functools

import jax
import jax.numpy as jnp
from jax import lax
from jax.experimental import pallas as pl
from jax.experimental.pallas import tpu as pltpu
from jax.sharding import PartitionSpec as P

RMAX = 4
STEPS = 2
INTERPRET = False
HI = lax.Precision.HIGHEST


def eliminate(right_of, k_ref, x_ref, r_ref):
    level_count = k_ref.shape[0]
    prev_ratio = None
    prev_scaled = None
    for level in range(level_count):
        right = right_of(level)
        lower_k = k_ref[level - 1] if level > 0 else None
        upper_k = k_ref[level] if level < level_count - 1 else None
        if level == 0:
            pivot_val = 1.0 + upper_k
            scaled = right / pivot_val
        else:
            diag_term = 1.0 + lower_k if upper_k is None else 1.0 + lower_k + upper_k
            pivot_val = diag_term + lower_k * prev_ratio
            scaled = (right + lower_k * prev_scaled) / pivot_val
        x_ref[level] = scaled
        if upper_k is not None:
            prev_ratio = -upper_k / pivot_val
            r_ref[level] = prev_ratio
        prev_scaled = scaled
    solved = prev_scaled
    for level in range(level_count - 2, -1, -1):
        solved = x_ref[level] - r_ref[level] * solved
        x_ref[level] = solved


def first_kernel(b_ref, k_ref, x_ref, r_ref):
    eliminate(lambda level: b_ref[level], k_ref, x_ref, r_ref)


def next_kernel(ep_ref, a_ref, s_ref, k_ref, x_ref, g_ref, r_ref):
    level_count = a_ref.shape[0]
    grad = ep_ref[0] * a_ref[0]
    for level in range(1, level_count):
        grad = grad + ep_ref[level] * a_ref[level]
    g_ref[...] = grad
    eliminate(lambda level: a_ref[level] * s_ref[level], k_ref, x_ref, r_ref)


def column_solve(mixing, right=None, ep=None, adjoint=None, survive=None):
    level_count, blocks, cells = mixing.shape
    chunk = 256
    spec = pl.BlockSpec((level_count, blocks, chunk), lambda c: (0, 0, c))
    scratch = [pltpu.VMEM((level_count, blocks, chunk), jnp.float32)]
    solved_shape = jax.ShapeDtypeStruct(mixing.shape, jnp.float32)
    if right is not None:
        return pl.pallas_call(
            first_kernel,
            grid=(cells // chunk,),
            in_specs=[spec, spec],
            out_specs=spec,
            out_shape=solved_shape,
            scratch_shapes=scratch,
            interpret=INTERPRET,
        )(right, mixing)
    return pl.pallas_call(
        next_kernel,
        grid=(cells // chunk,),
        in_specs=[pl.BlockSpec(memory_space=pltpu.SMEM), spec, spec, spec],
        out_specs=[spec, pl.BlockSpec((blocks, chunk), lambda c: (0, c))],
        out_shape=[solved_shape, jax.ShapeDtypeStruct((blocks, cells), jnp.float32)],
        scratch_shapes=scratch,
        interpret=INTERPRET,
    )(ep, adjoint, survive, mixing)


def stencil_kernel(side_len, st_ref, v_ref, e_ref, n_ref, o_ref):
    v = v_ref[...]
    east_c = e_ref[...]
    north_c = n_ref[...]
    cells = v.shape[1]
    lane = lax.broadcasted_iota(jnp.int32, v.shape, 1)
    east_ok = lane % side_len != side_len - 1
    north_ok = lane < cells - side_len
    keep = 1.0 - east_c - north_c
    steps = st_ref[...]
    for substep in range(RMAX):
        east_adj = jnp.where(east_ok, pltpu.roll(v, cells - 1, 1), 0.0)
        north_adj = jnp.where(north_ok, pltpu.roll(v, cells - side_len, 1), 0.0)
        moved = keep * v + east_c * east_adj + north_c * north_adj
        v = jnp.where(substep < steps, moved, v)
    o_ref[...] = v


def advect(side_len, steps, adjoint, east_c, north_c):
    rows, cells = adjoint.shape
    tile = 64
    spec = pl.BlockSpec((tile, cells), lambda r: (r, 0))
    return pl.pallas_call(
        functools.partial(stencil_kernel, side_len),
        grid=(rows // tile,),
        in_specs=[pl.BlockSpec((tile, 1), lambda r: (r, 0)), spec, spec, spec],
        out_specs=spec,
        out_shape=jax.ShapeDtypeStruct(adjoint.shape, jnp.float32),
        interpret=INTERPRET,
    )(steps, adjoint, east_c, north_c)


def face_matrix(side_len, cells):
    pos = jnp.arange(side_len, dtype=jnp.int32)
    where = jnp.concatenate([pos, (side_len - 1) * side_len + pos, pos * side_len, pos * side_len + side_len - 1])
    return (jnp.arange(cells, dtype=jnp.int32)[:, None] == where[None, :]).astype(jnp.float32)


def pack_plan(keys, dest_count, cap):
    count = keys.shape[0]
    order = jnp.arange(count, dtype=jnp.int32)
    earlier = (keys[:, None] == keys[None, :]) & (order[None, :] < order[:, None])
    slot = keys * cap + jnp.sum(earlier.astype(jnp.int32), axis=1)
    rows = jnp.arange(dest_count * cap, dtype=jnp.int32)
    return (rows[:, None] == slot[None, :]).astype(jnp.float32)


def to_columns(x):
    return lax.all_to_all(x, "lev", split_axis=x.ndim - 2, concat_axis=x.ndim - 3, tiled=True)


def ring_columns(x, lev_index, lev_groups):
    lead = x.shape[:-3]
    lev_dev, blocks, cells = x.shape[-3:]
    own = blocks // lev_groups
    parts = x.reshape(lead + (lev_dev, lev_groups, own, cells))
    got = []
    for shift in range(lev_groups):
        piece = lax.dynamic_index_in_dim(parts, (lev_index + shift) % lev_groups, axis=len(lead) + 1, keepdims=False)
        if shift:
            ring = [(src, (src + shift) % lev_groups) for src in range(lev_groups)]
            piece = lax.ppermute(piece, "lev", ring)
        got.append(piece)
    got = jnp.stack(got, axis=len(lead))
    order = (lev_index - jnp.arange(lev_groups, dtype=jnp.int32)) % lev_groups
    got = jnp.take(got, order, axis=len(lead))
    return got.reshape(lead + (lev_groups * lev_dev, own, cells))


def ring_exchange(x, lev_index, lev_groups):
    got = []
    for shift in range(lev_groups):
        piece = lax.dynamic_index_in_dim(x, (lev_index + shift) % lev_groups, axis=0, keepdims=False)
        if shift:
            ring = [(src, (src + shift) % lev_groups) for src in range(lev_groups)]
            piece = lax.ppermute(piece, "lev", ring)
        got.append(piece)
    got = jnp.stack(got, axis=0)
    order = (lev_index - jnp.arange(lev_groups, dtype=jnp.int32)) % lev_groups
    return jnp.take(got, order, axis=0)


def ring_sum(x, lev_index, lev_groups):
    total = lax.dynamic_index_in_dim(x, lev_index, axis=0, keepdims=False)
    for shift in range(1, lev_groups):
        piece = lax.dynamic_index_in_dim(x, (lev_index + shift) % lev_groups, axis=0, keepdims=False)
        ring = [(src, (src + shift) % lev_groups) for src in range(lev_groups)]
        total = total + lax.ppermute(piece, "lev", ring)
    return total


def local(
    adjoint_in,
    courant,
    mixing,
    oh_rate,
    substeps,
    nest_weight,
    dest_device,
    dest_slot,
    emission_profile,
    tile_owner,
):
    blocks, lev_dev, cell_count = adjoint_in.shape
    cycle_len = nest_weight.shape[1]
    side_len = cycle_len // 4
    peer_count = lax.axis_size("blk")
    lev_groups = lax.axis_size("lev")
    lev_index = lax.axis_index("lev")
    own = blocks // lev_groups
    levels = lev_dev * lev_groups
    cap = 2

    survive = jnp.exp(-oh_rate)
    state = to_columns(jnp.stack([adjoint_in * survive, mixing]).transpose(0, 2, 1, 3))
    right, column_mixing = state[0], state[1]
    ep = jnp.broadcast_to(emission_profile[:, None, None], (lev_dev, lev_groups, 1))
    ep = ring_columns(ep, lev_index, lev_groups).reshape(levels)
    deferred = (courant.transpose(0, 2, 1, 3), survive.transpose(1, 0, 2))
    grad_sum = jnp.sum(adjoint_in * emission_profile[None, :, None], axis=1)

    own_steps = lax.dynamic_slice_in_dim(substeps, lev_index * own, own)
    row_steps = jnp.tile(own_steps, levels)[:, None]
    own_weight = lax.dynamic_slice_in_dim(nest_weight, lev_index * own, own)

    face_pack = pack_plan(dest_device[:, 0], peer_count, cap)
    tiles_total = blocks * peer_count // 4
    group_size = tiles_total // peer_count
    tile_pack = pack_plan(tile_owner // group_size, peer_count, cap)
    info = jnp.stack(
        [
            jnp.dot(face_pack, (dest_slot + 1).astype(jnp.float32), precision=HI),
            jnp.dot(tile_pack, (tile_owner % group_size + 1).astype(jnp.float32), precision=HI),
        ],
        axis=1,
    )
    info = jnp.pad(info, ((0, 0), (0, cycle_len - 2))).reshape(peer_count, cap, cycle_len)
    face_width = lev_dev * cycle_len

    pick = face_matrix(side_len, cell_count)
    for step_index in range(STEPS):
        if step_index == 0:
            solved = column_solve(column_mixing, right=right)
            deferred, solved = lax.optimization_barrier((deferred, solved))
            flows = ring_columns(deferred[0], lev_index, lev_groups).reshape(2, levels * own, cell_count)
            column_survive = ring_columns(deferred[1], lev_index, lev_groups)
        else:
            solved, grad_step = column_solve(column_mixing, ep=ep, adjoint=adjoint, survive=column_survive)
            mine = lax.dynamic_slice_in_dim(grad_sum, lev_index * own, own)
            grad_sum = lax.dynamic_update_slice_in_dim(grad_sum, mine + grad_step, lev_index * own, 0)
        flat = solved.reshape(levels * own, cell_count)
        cycle_out = jnp.dot(flat, pick, precision=HI).reshape(levels, own, cycle_len) * own_weight[None]
        by_level = lax.all_to_all(cycle_out, "lev", split_axis=0, concat_axis=1, tiled=True)
        sent = jnp.einsum("sb,lbk->slk", face_pack, by_level, precision=HI)
        sent = sent.reshape(peer_count, cap, face_width)
        if step_index == 0:
            sent = jnp.concatenate([sent, info], axis=2)
        if step_index == STEPS - 1:
            quarter = grad_sum.reshape(blocks, lev_groups, cell_count // lev_groups).transpose(1, 0, 2)
            quarter = ring_sum(quarter, lev_index, lev_groups)
            tile_sent = jnp.dot(tile_pack, quarter, precision=HI).reshape(peer_count, cap, -1)
            sent = jnp.concatenate([sent, tile_sent], axis=2)
        got = lax.all_to_all(sent, "blk", split_axis=0, concat_axis=0, tiled=True)
        got = got.reshape(peer_count * cap, -1)
        if step_index == 0:
            face_take = (
                got[:, face_width][None, :]
                == (jnp.arange(blocks, dtype=jnp.int32) + 1).astype(jnp.float32)[:, None]
            ).astype(jnp.float32)
            tile_take = (
                got[:, face_width + 1][None, :]
                == (jnp.arange(group_size, dtype=jnp.int32) + 1).astype(jnp.float32)[:, None]
            ).astype(jnp.float32)
        if step_index == STEPS - 1:
            tile_got = got[:, face_width:]
        got = got[:, :face_width].reshape(peer_count * cap, lev_dev, cycle_len)
        arrivals = jnp.einsum("ts,slk->ltk", face_take, got, precision=HI)
        advected = advect(side_len, row_steps, flat, flows[0], flows[1])
        if step_index < STEPS - 1:
            arrivals = to_columns(arrivals).reshape(levels * own, cycle_len)
            added = jnp.dot(arrivals, pick.T, precision=HI)
            adjoint = (advected + added).reshape(levels, own, cell_count)

    by_dest = advected.reshape(lev_groups, lev_dev, own, cell_count)
    by_src = ring_exchange(by_dest, lev_index, lev_groups)
    advected = by_src.transpose(1, 0, 2, 3).reshape(lev_dev, blocks, cell_count)
    added = jnp.dot(arrivals.reshape(lev_dev * blocks, cycle_len), pick.T, precision=HI)
    adjoint_out = (advected + added.reshape(lev_dev, blocks, cell_count)).transpose(1, 0, 2)

    tile_parts = jnp.dot(tile_take, tile_got, precision=HI)
    tile_rows = group_size // lev_groups
    tile_parts = tile_parts.reshape(lev_groups, tile_rows, cell_count // lev_groups)
    tile_grad = ring_exchange(tile_parts, lev_index, lev_groups)
    tile_grad = tile_grad.transpose(1, 0, 2).reshape(tile_rows, cell_count)
    return (adjoint_out, tile_grad)


def solution(mesh):
    placed = (
        P("blk", "lev", None),
        P(None, "blk", "lev", None),
        P("blk", "lev", None),
        P("blk", "lev", None),
        P("blk"),
        P("blk", None),
        P("blk", None),
        P("blk"),
        P("lev"),
        P("blk"),
    )
    return jax.shard_map(
        local,
        mesh=mesh,
        in_specs=placed,
        out_specs=(P("blk", "lev", None), P(("blk", "lev"), None)),
        check_vma=False,
    )
```

```python
import functools

import jax
import jax.numpy as jnp
from jax import lax
from jax.experimental import pallas as pl
from jax.experimental.pallas import tpu as pltpu
from jax.sharding import PartitionSpec as P

RMAX = 4
STEPS = 2
INTERPRET = False
HI = lax.Precision.HIGHEST


def eliminate(right_of, k_ref, x_ref, r_ref):
    level_count = k_ref.shape[0]
    prev_ratio = None
    prev_scaled = None
    for level in range(level_count):
        right = right_of(level)
        lower_k = k_ref[level - 1] if level > 0 else None
        upper_k = k_ref[level] if level < level_count - 1 else None
        if level == 0:
            pivot_val = 1.0 + upper_k
            scaled = right / pivot_val
        else:
            diag_term = 1.0 + lower_k if upper_k is None else 1.0 + lower_k + upper_k
            pivot_val = diag_term + lower_k * prev_ratio
            scaled = (right + lower_k * prev_scaled) / pivot_val
        x_ref[level] = scaled
        if upper_k is not None:
            prev_ratio = -upper_k / pivot_val
            r_ref[level] = prev_ratio
        prev_scaled = scaled
    solved = prev_scaled
    for level in range(level_count - 2, -1, -1):
        solved = x_ref[level] - r_ref[level] * solved
        x_ref[level] = solved


def first_kernel(b_ref, k_ref, x_ref, r_ref):
    eliminate(lambda level: b_ref[level], k_ref, x_ref, r_ref)


def next_kernel(ep_ref, a_ref, s_ref, k_ref, x_ref, g_ref, r_ref):
    level_count = a_ref.shape[0]
    grad = ep_ref[0] * a_ref[0]
    for level in range(1, level_count):
        grad = grad + ep_ref[level] * a_ref[level]
    g_ref[...] = grad
    eliminate(lambda level: a_ref[level] * s_ref[level], k_ref, x_ref, r_ref)


def column_solve(mixing, right=None, ep=None, adjoint=None, survive=None):
    level_count, blocks, cells = mixing.shape
    chunk = 256
    spec = pl.BlockSpec((level_count, blocks, chunk), lambda c: (0, 0, c))
    scratch = [pltpu.VMEM((level_count, blocks, chunk), jnp.float32)]
    solved_shape = jax.ShapeDtypeStruct(mixing.shape, jnp.float32)
    if right is not None:
        return pl.pallas_call(
            first_kernel,
            grid=(cells // chunk,),
            in_specs=[spec, spec],
            out_specs=spec,
            out_shape=solved_shape,
            scratch_shapes=scratch,
            interpret=INTERPRET,
        )(right, mixing)
    return pl.pallas_call(
        next_kernel,
        grid=(cells // chunk,),
        in_specs=[pl.BlockSpec(memory_space=pltpu.SMEM), spec, spec, spec],
        out_specs=[spec, pl.BlockSpec((blocks, chunk), lambda c: (0, c))],
        out_shape=[solved_shape, jax.ShapeDtypeStruct((blocks, cells), jnp.float32)],
        scratch_shapes=scratch,
        interpret=INTERPRET,
    )(ep, adjoint, survive, mixing)


def stencil_kernel(side_len, st_ref, v_ref, e_ref, n_ref, o_ref):
    v = v_ref[...]
    east_c = e_ref[...]
    north_c = n_ref[...]
    cells = v.shape[1]
    lane = lax.broadcasted_iota(jnp.int32, v.shape, 1)
    east_ok = lane % side_len != side_len - 1
    north_ok = lane < cells - side_len
    keep = 1.0 - east_c - north_c
    east_c = jnp.where(east_ok, east_c, 0.0)
    north_c = jnp.where(north_ok, north_c, 0.0)
    steps = st_ref[...]
    for substep in range(RMAX):
        east_adj = pltpu.roll(v, cells - 1, 1)
        north_adj = pltpu.roll(v, cells - side_len, 1)
        moved = keep * v + east_c * east_adj + north_c * north_adj
        v = jnp.where(substep < steps, moved, v)
    o_ref[...] = v


def advect(side_len, steps, adjoint, east_c, north_c):
    rows, cells = adjoint.shape
    tile = 64
    spec = pl.BlockSpec((tile, cells), lambda r: (r, 0))
    return pl.pallas_call(
        functools.partial(stencil_kernel, side_len),
        grid=(rows // tile,),
        in_specs=[pl.BlockSpec((tile, 1), lambda r: (r, 0)), spec, spec, spec],
        out_specs=spec,
        out_shape=jax.ShapeDtypeStruct(adjoint.shape, jnp.float32),
        interpret=INTERPRET,
    )(steps, adjoint, east_c, north_c)


def face_matrix(side_len, cells):
    pos = jnp.arange(side_len, dtype=jnp.int32)
    where = jnp.concatenate([pos, (side_len - 1) * side_len + pos, pos * side_len, pos * side_len + side_len - 1])
    return (jnp.arange(cells, dtype=jnp.int32)[:, None] == where[None, :]).astype(jnp.float32)


def pack_plan(keys, dest_count, cap):
    count = keys.shape[0]
    order = jnp.arange(count, dtype=jnp.int32)
    earlier = (keys[:, None] == keys[None, :]) & (order[None, :] < order[:, None])
    slot = keys * cap + jnp.sum(earlier.astype(jnp.int32), axis=1)
    rows = jnp.arange(dest_count * cap, dtype=jnp.int32)
    return (rows[:, None] == slot[None, :]).astype(jnp.float32)


def to_columns(x):
    return lax.all_to_all(x, "lev", split_axis=x.ndim - 2, concat_axis=x.ndim - 3, tiled=True)


def ring_columns(x, lev_index, lev_groups):
    lead = x.shape[:-3]
    lev_dev, blocks, cells = x.shape[-3:]
    own = blocks // lev_groups
    parts = x.reshape(lead + (lev_dev, lev_groups, own, cells))
    got = []
    for shift in range(lev_groups):
        piece = lax.dynamic_index_in_dim(parts, (lev_index + shift) % lev_groups, axis=len(lead) + 1, keepdims=False)
        if shift:
            ring = [(src, (src + shift) % lev_groups) for src in range(lev_groups)]
            piece = lax.ppermute(piece, "lev", ring)
        got.append(piece)
    got = jnp.stack(got, axis=len(lead))
    order = (lev_index - jnp.arange(lev_groups, dtype=jnp.int32)) % lev_groups
    got = jnp.take(got, order, axis=len(lead))
    return got.reshape(lead + (lev_groups * lev_dev, own, cells))


def ring_exchange(x, lev_index, lev_groups):
    got = []
    for shift in range(lev_groups):
        piece = lax.dynamic_index_in_dim(x, (lev_index + shift) % lev_groups, axis=0, keepdims=False)
        if shift:
            ring = [(src, (src + shift) % lev_groups) for src in range(lev_groups)]
            piece = lax.ppermute(piece, "lev", ring)
        got.append(piece)
    got = jnp.stack(got, axis=0)
    order = (lev_index - jnp.arange(lev_groups, dtype=jnp.int32)) % lev_groups
    return jnp.take(got, order, axis=0)


def ring_sum(x, lev_index, lev_groups):
    total = lax.dynamic_index_in_dim(x, lev_index, axis=0, keepdims=False)
    for shift in range(1, lev_groups):
        piece = lax.dynamic_index_in_dim(x, (lev_index + shift) % lev_groups, axis=0, keepdims=False)
        ring = [(src, (src + shift) % lev_groups) for src in range(lev_groups)]
        total = total + lax.ppermute(piece, "lev", ring)
    return total


def local(
    adjoint_in,
    courant,
    mixing,
    oh_rate,
    substeps,
    nest_weight,
    dest_device,
    dest_slot,
    emission_profile,
    tile_owner,
):
    blocks, lev_dev, cell_count = adjoint_in.shape
    cycle_len = nest_weight.shape[1]
    side_len = cycle_len // 4
    peer_count = lax.axis_size("blk")
    lev_groups = lax.axis_size("lev")
    lev_index = lax.axis_index("lev")
    own = blocks // lev_groups
    levels = lev_dev * lev_groups
    cap = 2

    survive = jnp.exp(-oh_rate)
    state = to_columns(jnp.stack([adjoint_in * survive, mixing]).transpose(0, 2, 1, 3))
    right, column_mixing = state[0], state[1]
    ep = jnp.broadcast_to(emission_profile[:, None, None], (lev_dev, lev_groups, 1))
    ep = ring_columns(ep, lev_index, lev_groups).reshape(levels)
    deferred = (courant.transpose(0, 2, 1, 3), survive.transpose(1, 0, 2))
    grad_sum = jnp.sum(adjoint_in * emission_profile[None, :, None], axis=1)

    own_steps = lax.dynamic_slice_in_dim(substeps, lev_index * own, own)
    row_steps = jnp.tile(own_steps, levels)[:, None]
    own_weight = lax.dynamic_slice_in_dim(nest_weight, lev_index * own, own)

    face_pack = pack_plan(dest_device[:, 0], peer_count, cap)
    tiles_total = blocks * peer_count // 4
    group_size = tiles_total // peer_count
    tile_pack = pack_plan(tile_owner // group_size, peer_count, cap)
    info = jnp.stack(
        [
            jnp.dot(face_pack, (dest_slot + 1).astype(jnp.float32), precision=HI),
            jnp.dot(tile_pack, (tile_owner % group_size + 1).astype(jnp.float32), precision=HI),
        ],
        axis=1,
    )
    info = jnp.pad(info, ((0, 0), (0, cycle_len - 2))).reshape(peer_count, cap, cycle_len)
    face_width = lev_dev * cycle_len

    pick = face_matrix(side_len, cell_count)
    for step_index in range(STEPS):
        if step_index == 0:
            solved = column_solve(column_mixing, right=right)
            deferred, solved = lax.optimization_barrier((deferred, solved))
            flows = ring_columns(deferred[0], lev_index, lev_groups).reshape(2, levels * own, cell_count)
            column_survive = ring_columns(deferred[1], lev_index, lev_groups)
        else:
            solved, grad_step = column_solve(column_mixing, ep=ep, adjoint=adjoint, survive=column_survive)
            mine = lax.dynamic_slice_in_dim(grad_sum, lev_index * own, own)
            grad_sum = lax.dynamic_update_slice_in_dim(grad_sum, mine + grad_step, lev_index * own, 0)
        flat = solved.reshape(levels * own, cell_count)
        cycle_out = jnp.dot(flat, pick, precision=HI).reshape(levels, own, cycle_len) * own_weight[None]
        by_level = lax.all_to_all(cycle_out, "lev", split_axis=0, concat_axis=1, tiled=True)
        sent = jnp.einsum("sb,lbk->slk", face_pack, by_level, precision=HI)
        sent = sent.reshape(peer_count, cap, face_width)
        if step_index == 0:
            sent = jnp.concatenate([sent, info], axis=2)
        if step_index == STEPS - 1:
            quarter = grad_sum.reshape(blocks, lev_groups, cell_count // lev_groups).transpose(1, 0, 2)
            quarter = ring_sum(quarter, lev_index, lev_groups)
            tile_sent = jnp.dot(tile_pack, quarter, precision=HI).reshape(peer_count, cap, -1)
            sent = jnp.concatenate([sent, tile_sent], axis=2)
        got = lax.all_to_all(sent, "blk", split_axis=0, concat_axis=0, tiled=True)
        got = got.reshape(peer_count * cap, -1)
        if step_index == 0:
            face_take = (
                got[:, face_width][None, :]
                == (jnp.arange(blocks, dtype=jnp.int32) + 1).astype(jnp.float32)[:, None]
            ).astype(jnp.float32)
            tile_take = (
                got[:, face_width + 1][None, :]
                == (jnp.arange(group_size, dtype=jnp.int32) + 1).astype(jnp.float32)[:, None]
            ).astype(jnp.float32)
        if step_index == STEPS - 1:
            tile_got = got[:, face_width:]
        got = got[:, :face_width].reshape(peer_count * cap, lev_dev, cycle_len)
        arrivals = jnp.einsum("ts,slk->ltk", face_take, got, precision=HI)
        advected = advect(side_len, row_steps, flat, flows[0], flows[1])
        if step_index < STEPS - 1:
            arrivals = to_columns(arrivals).reshape(levels * own, cycle_len)
            added = jnp.dot(arrivals, pick.T, precision=HI)
            adjoint = (advected + added).reshape(levels, own, cell_count)

    by_dest = advected.reshape(lev_groups, lev_dev, own, cell_count)
    by_src = ring_exchange(by_dest, lev_index, lev_groups)
    advected = by_src.transpose(1, 0, 2, 3).reshape(lev_dev, blocks, cell_count)
    added = jnp.dot(arrivals.reshape(lev_dev * blocks, cycle_len), pick.T, precision=HI)
    adjoint_out = (advected + added.reshape(lev_dev, blocks, cell_count)).transpose(1, 0, 2)

    tile_parts = jnp.dot(tile_take, tile_got, precision=HI)
    tile_rows = group_size // lev_groups
    tile_parts = tile_parts.reshape(lev_groups, tile_rows, cell_count // lev_groups)
    tile_grad = ring_exchange(tile_parts, lev_index, lev_groups)
    tile_grad = tile_grad.transpose(1, 0, 2).reshape(tile_rows, cell_count)
    return (adjoint_out, tile_grad)


def solution(mesh):
    placed = (
        P("blk", "lev", None),
        P(None, "blk", "lev", None),
        P("blk", "lev", None),
        P("blk", "lev", None),
        P("blk"),
        P("blk", None),
        P("blk", None),
        P("blk"),
        P("lev"),
        P("blk"),
    )
    return jax.shard_map(
        local,
        mesh=mesh,
        in_specs=placed,
        out_specs=(P("blk", "lev", None), P(("blk", "lev"), None)),
        check_vma=False,
    )
```

```python
import functools

import jax
import jax.numpy as jnp
from jax import lax
from jax.experimental import pallas as pl
from jax.experimental.pallas import tpu as pltpu
from jax.sharding import PartitionSpec as P

RMAX = 4
STEPS = 2
INTERPRET = False
HI = lax.Precision.HIGHEST


def eliminate(right_of, k_ref, x_ref, r_ref):
    level_count = k_ref.shape[0]
    prev_ratio = None
    prev_scaled = None
    for level in range(level_count):
        right = right_of(level)
        lower_k = k_ref[level - 1] if level > 0 else None
        upper_k = k_ref[level] if level < level_count - 1 else None
        if level == 0:
            pivot_val = 1.0 + upper_k
            scaled = right / pivot_val
        else:
            diag_term = 1.0 + lower_k if upper_k is None else 1.0 + lower_k + upper_k
            pivot_val = diag_term + lower_k * prev_ratio
            scaled = (right + lower_k * prev_scaled) / pivot_val
        x_ref[level] = scaled
        if upper_k is not None:
            prev_ratio = -upper_k / pivot_val
            r_ref[level] = prev_ratio
        prev_scaled = scaled
    solved = prev_scaled
    for level in range(level_count - 2, -1, -1):
        solved = x_ref[level] - r_ref[level] * solved
        x_ref[level] = solved


def first_kernel(b_ref, k_ref, x_ref, r_ref):
    eliminate(lambda level: b_ref[level], k_ref, x_ref, r_ref)


def next_kernel(ep_ref, a_ref, s_ref, k_ref, x_ref, g_ref, r_ref):
    level_count = a_ref.shape[0]
    grad = ep_ref[0] * a_ref[0]
    for level in range(1, level_count):
        grad = grad + ep_ref[level] * a_ref[level]
    g_ref[...] = grad
    eliminate(lambda level: a_ref[level] * s_ref[level], k_ref, x_ref, r_ref)


def column_solve(mixing, right=None, ep=None, adjoint=None, survive=None):
    level_count, blocks, cells = mixing.shape
    chunk = 512
    spec = pl.BlockSpec((level_count, blocks, chunk), lambda c: (0, 0, c))
    scratch = [pltpu.VMEM((level_count, blocks, chunk), jnp.float32)]
    solved_shape = jax.ShapeDtypeStruct(mixing.shape, jnp.float32)
    if right is not None:
        return pl.pallas_call(
            first_kernel,
            grid=(cells // chunk,),
            in_specs=[spec, spec],
            out_specs=spec,
            out_shape=solved_shape,
            scratch_shapes=scratch,
            interpret=INTERPRET,
        )(right, mixing)
    return pl.pallas_call(
        next_kernel,
        grid=(cells // chunk,),
        in_specs=[pl.BlockSpec(memory_space=pltpu.SMEM), spec, spec, spec],
        out_specs=[spec, pl.BlockSpec((blocks, chunk), lambda c: (0, c))],
        out_shape=[solved_shape, jax.ShapeDtypeStruct((blocks, cells), jnp.float32)],
        scratch_shapes=scratch,
        interpret=INTERPRET,
    )(ep, adjoint, survive, mixing)


def stencil_kernel(side_len, st_ref, v_ref, e_ref, n_ref, o_ref):
    v = v_ref[...]
    east_c = e_ref[...]
    north_c = n_ref[...]
    cells = v.shape[1]
    lane = lax.broadcasted_iota(jnp.int32, v.shape, 1)
    east_ok = lane % side_len != side_len - 1
    north_ok = lane < cells - side_len
    keep = 1.0 - east_c - north_c
    steps = st_ref[...]
    for substep in range(RMAX):
        east_adj = jnp.where(east_ok, pltpu.roll(v, cells - 1, 1), 0.0)
        north_adj = jnp.where(north_ok, pltpu.roll(v, cells - side_len, 1), 0.0)
        moved = keep * v + east_c * east_adj + north_c * north_adj
        v = jnp.where(substep < steps, moved, v)
    o_ref[...] = v


def advect(side_len, steps, adjoint, east_c, north_c):
    rows, cells = adjoint.shape
    tile = 96
    spec = pl.BlockSpec((tile, cells), lambda r: (r, 0))
    return pl.pallas_call(
        functools.partial(stencil_kernel, side_len),
        grid=(rows // tile,),
        in_specs=[pl.BlockSpec((tile, 1), lambda r: (r, 0)), spec, spec, spec],
        out_specs=spec,
        out_shape=jax.ShapeDtypeStruct(adjoint.shape, jnp.float32),
        interpret=INTERPRET,
    )(steps, adjoint, east_c, north_c)


def face_matrix(side_len, cells):
    pos = jnp.arange(side_len, dtype=jnp.int32)
    where = jnp.concatenate([pos, (side_len - 1) * side_len + pos, pos * side_len, pos * side_len + side_len - 1])
    return (jnp.arange(cells, dtype=jnp.int32)[:, None] == where[None, :]).astype(jnp.float32)


def pack_plan(keys, dest_count, cap):
    count = keys.shape[0]
    order = jnp.arange(count, dtype=jnp.int32)
    earlier = (keys[:, None] == keys[None, :]) & (order[None, :] < order[:, None])
    slot = keys * cap + jnp.sum(earlier.astype(jnp.int32), axis=1)
    rows = jnp.arange(dest_count * cap, dtype=jnp.int32)
    return (rows[:, None] == slot[None, :]).astype(jnp.float32)


def to_columns(x):
    return lax.all_to_all(x, "lev", split_axis=x.ndim - 2, concat_axis=x.ndim - 3, tiled=True)


def ring_columns(x, lev_index, lev_groups):
    lead = x.shape[:-3]
    lev_dev, blocks, cells = x.shape[-3:]
    own = blocks // lev_groups
    parts = x.reshape(lead + (lev_dev, lev_groups, own, cells))
    got = []
    for shift in range(lev_groups):
        piece = lax.dynamic_index_in_dim(parts, (lev_index + shift) % lev_groups, axis=len(lead) + 1, keepdims=False)
        if shift:
            ring = [(src, (src + shift) % lev_groups) for src in range(lev_groups)]
            piece = lax.ppermute(piece, "lev", ring)
        got.append(piece)
    got = jnp.stack(got, axis=len(lead))
    order = (lev_index - jnp.arange(lev_groups, dtype=jnp.int32)) % lev_groups
    got = jnp.take(got, order, axis=len(lead))
    return got.reshape(lead + (lev_groups * lev_dev, own, cells))


def ring_exchange(x, lev_index, lev_groups):
    got = []
    for shift in range(lev_groups):
        piece = lax.dynamic_index_in_dim(x, (lev_index + shift) % lev_groups, axis=0, keepdims=False)
        if shift:
            ring = [(src, (src + shift) % lev_groups) for src in range(lev_groups)]
            piece = lax.ppermute(piece, "lev", ring)
        got.append(piece)
    got = jnp.stack(got, axis=0)
    order = (lev_index - jnp.arange(lev_groups, dtype=jnp.int32)) % lev_groups
    return jnp.take(got, order, axis=0)


def ring_sum(x, lev_index, lev_groups):
    total = lax.dynamic_index_in_dim(x, lev_index, axis=0, keepdims=False)
    for shift in range(1, lev_groups):
        piece = lax.dynamic_index_in_dim(x, (lev_index + shift) % lev_groups, axis=0, keepdims=False)
        ring = [(src, (src + shift) % lev_groups) for src in range(lev_groups)]
        total = total + lax.ppermute(piece, "lev", ring)
    return total


def local(
    adjoint_in,
    courant,
    mixing,
    oh_rate,
    substeps,
    nest_weight,
    dest_device,
    dest_slot,
    emission_profile,
    tile_owner,
):
    blocks, lev_dev, cell_count = adjoint_in.shape
    cycle_len = nest_weight.shape[1]
    side_len = cycle_len // 4
    peer_count = lax.axis_size("blk")
    lev_groups = lax.axis_size("lev")
    lev_index = lax.axis_index("lev")
    own = blocks // lev_groups
    levels = lev_dev * lev_groups
    cap = 2

    survive = jnp.exp(-oh_rate)
    state = to_columns(jnp.stack([adjoint_in * survive, mixing]).transpose(0, 2, 1, 3))
    right, column_mixing = state[0], state[1]
    ep = jnp.broadcast_to(emission_profile[:, None, None], (lev_dev, lev_groups, 1))
    ep = ring_columns(ep, lev_index, lev_groups).reshape(levels)
    deferred = (courant.transpose(0, 2, 1, 3), survive.transpose(1, 0, 2))
    grad_sum = jnp.sum(adjoint_in * emission_profile[None, :, None], axis=1)

    own_steps = lax.dynamic_slice_in_dim(substeps, lev_index * own, own)
    row_steps = jnp.tile(own_steps, levels)[:, None]
    own_weight = lax.dynamic_slice_in_dim(nest_weight, lev_index * own, own)

    face_pack = pack_plan(dest_device[:, 0], peer_count, cap)
    tiles_total = blocks * peer_count // 4
    group_size = tiles_total // peer_count
    tile_pack = pack_plan(tile_owner // group_size, peer_count, cap)
    info = jnp.stack(
        [
            jnp.dot(face_pack, (dest_slot + 1).astype(jnp.float32), precision=HI),
            jnp.dot(tile_pack, (tile_owner % group_size + 1).astype(jnp.float32), precision=HI),
        ],
        axis=1,
    )
    info = jnp.pad(info, ((0, 0), (0, cycle_len - 2))).reshape(peer_count, cap, cycle_len)
    face_width = lev_dev * cycle_len

    pick = face_matrix(side_len, cell_count)
    for step_index in range(STEPS):
        if step_index == 0:
            solved = column_solve(column_mixing, right=right)
            deferred, solved = lax.optimization_barrier((deferred, solved))
            flows = ring_columns(deferred[0], lev_index, lev_groups).reshape(2, levels * own, cell_count)
            column_survive = ring_columns(deferred[1], lev_index, lev_groups)
        else:
            solved, grad_step = column_solve(column_mixing, ep=ep, adjoint=adjoint, survive=column_survive)
            mine = lax.dynamic_slice_in_dim(grad_sum, lev_index * own, own)
            grad_sum = lax.dynamic_update_slice_in_dim(grad_sum, mine + grad_step, lev_index * own, 0)
        flat = solved.reshape(levels * own, cell_count)
        cycle_out = jnp.dot(flat, pick, precision=HI).reshape(levels, own, cycle_len) * own_weight[None]
        by_level = lax.all_to_all(cycle_out, "lev", split_axis=0, concat_axis=1, tiled=True)
        sent = jnp.einsum("sb,lbk->slk", face_pack, by_level, precision=HI)
        sent = sent.reshape(peer_count, cap, face_width)
        if step_index == 0:
            sent = jnp.concatenate([sent, info], axis=2)
        if step_index == STEPS - 1:
            quarter = grad_sum.reshape(blocks, lev_groups, cell_count // lev_groups).transpose(1, 0, 2)
            quarter = ring_sum(quarter, lev_index, lev_groups)
            tile_sent = jnp.dot(tile_pack, quarter, precision=HI).reshape(peer_count, cap, -1)
            sent = jnp.concatenate([sent, tile_sent], axis=2)
        got = lax.all_to_all(sent, "blk", split_axis=0, concat_axis=0, tiled=True)
        got = got.reshape(peer_count * cap, -1)
        if step_index == 0:
            face_take = (
                got[:, face_width][None, :]
                == (jnp.arange(blocks, dtype=jnp.int32) + 1).astype(jnp.float32)[:, None]
            ).astype(jnp.float32)
            tile_take = (
                got[:, face_width + 1][None, :]
                == (jnp.arange(group_size, dtype=jnp.int32) + 1).astype(jnp.float32)[:, None]
            ).astype(jnp.float32)
        if step_index == STEPS - 1:
            tile_got = got[:, face_width:]
        got = got[:, :face_width].reshape(peer_count * cap, lev_dev, cycle_len)
        arrivals = jnp.einsum("ts,slk->ltk", face_take, got, precision=HI)
        advected = advect(side_len, row_steps, flat, flows[0], flows[1])
        if step_index < STEPS - 1:
            arrivals = to_columns(arrivals).reshape(levels * own, cycle_len)
            added = jnp.dot(arrivals, pick.T, precision=HI)
            adjoint = (advected + added).reshape(levels, own, cell_count)

    by_dest = advected.reshape(lev_groups, lev_dev, own, cell_count)
    by_src = ring_exchange(by_dest, lev_index, lev_groups)
    advected = by_src.transpose(1, 0, 2, 3).reshape(lev_dev, blocks, cell_count)
    added = jnp.dot(arrivals.reshape(lev_dev * blocks, cycle_len), pick.T, precision=HI)
    adjoint_out = (advected + added.reshape(lev_dev, blocks, cell_count)).transpose(1, 0, 2)

    tile_parts = jnp.dot(tile_take, tile_got, precision=HI)
    tile_rows = group_size // lev_groups
    tile_parts = tile_parts.reshape(lev_groups, tile_rows, cell_count // lev_groups)
    tile_grad = ring_exchange(tile_parts, lev_index, lev_groups)
    tile_grad = tile_grad.transpose(1, 0, 2).reshape(tile_rows, cell_count)
    return (adjoint_out, tile_grad)


def solution(mesh):
    placed = (
        P("blk", "lev", None),
        P(None, "blk", "lev", None),
        P("blk", "lev", None),
        P("blk", "lev", None),
        P("blk"),
        P("blk", None),
        P("blk", None),
        P("blk"),
        P("lev"),
        P("blk"),
    )
    return jax.shard_map(
        local,
        mesh=mesh,
        in_specs=placed,
        out_specs=(P("blk", "lev", None), P(("blk", "lev"), None)),
        check_vma=False,
    )
```
